32 devices in a mesh: groups: 2 (over y), tiles: 4 (over z), band: 2 (over x), rep: 2 (over core).
Axes of the slice: x: 2, y: 2, z: 4, core: 2. Of those that a mesh axis runs over, the one named last changes fastest.
Arguments:
- features: bfloat16 [8, 16, 2, 16, 128], P(('groups', 'band'), 'tiles'), parts along dimension 0, may hold values from -6 to 6
- state: float32 [8, 16, 16, 16, 128], P(('groups', 'band'), 'tiles'), parts along dimension 0, may hold values from -3 to 3
- live: int32 [16], P('tiles'), may hold values from 0 to 1, as said below
- neighbours: int32 [16, 2], P('tiles'), may hold values from -1 to 15, as said below
- coarse_perm: int32 [4, 4], P('tiles'), may hold values from 0 to 3, as said below
- coarse_state: float32 [32, 16, 4, 32], P(('groups', 'tiles', 'band')), parts along dimension 0, may hold values from -3 to 3
- w_update: bfloat16 [9, 16, 18], replicated, may hold values from -0.5 to 0.5
- b_update: float32 [16], replicated, may hold values from -3 to 3
- w_reset: bfloat16 [9, 16, 18], replicated, may hold values from -0.5 to 0.5
- b_reset: float32 [16], replicated, may hold values from -3 to 3
- w_cand: bfloat16 [9, 16, 18], replicated, may hold values from -0.5 to 0.5
- b_cand: float32 [16], replicated, may hold values from -3 to 3
- u_pool: float32 [16, 16], replicated, may hold values from -1.5 to 1.5
- u_state: float32 [16, 16], replicated, may hold values from -1.5 to 1.5
- b_coarse: float32 [16], replicated, may hold values from -3 to 3
Outputs:
- new_state: float32 [8, 16, 16, 16, 128], P(('groups', 'band'), 'tiles', 'rep'), parts along dimension 0
- coarse_next: float32 [32, 16, 4, 32], P(('groups', 'tiles', 'band')), parts along dimension 0
The draws below stay inside these ranges and needn't reach their ends.
There are 2 independent parts, one for each index of `groups`. The reference program is written for one: setup_inputs(seed, part) draws one part's arguments, and reference() takes and returns one part's arrays. A program takes and returns all parts, laid end to end along the dimension named above; an argument that names none is the same for every part. Nothing has to cross between parts.
Inputs may be any that keep to these rules, and one draw needn't show every extreme that they name: Every device of tiles has between 1 and 4 live slots, at any positions; in every draw some device has all 4 live. `neighbours`: the live tiles form one vertical chain that passes the devices of tiles in index order, each device's live tiles forming one run of the chain in some order; entry 0 names the tile above, entry 1 the tile below, -1 at the chain's two ends and in both entries of an empty slot. `coarse_perm`: each row is a permutation of 0 to 3.
All inputs are finite; a program needn't handle non-finite values.
Results may differ from the reference program's by a relative error of at most 0.0013.
Values may be sent and summed in bfloat16 or wider, within the bound.
No kernel may reach another device: no remote copies, remote signals or barrier semaphores. Data moves between devices by JAX's collectives and lax.ppermute only.
A program may use at most 64 MiB of HBM per device.

```python
import jax
import jax.numpy as jnp
from jax import lax

C = 16
XC = 2
TR = 16
W = 128
SLOTS = 4
BANDS = 4
SLOTS_ALL = 16
CR = 4
CW = 32
N_TILES = 4


def build_chain(key):
    k_count, k_busy, k_order = jax.random.split(jax.random.fold_in(key, 11), 3)
    counts = jax.random.randint(k_count, (N_TILES,), 1, SLOTS + 1).astype(jnp.int32)
    busiest = jax.random.randint(k_busy, (), 0, N_TILES).astype(jnp.int32)
    counts = jnp.where(jnp.arange(N_TILES, dtype=jnp.int32) == busiest, SLOTS, counts)
    orders = jax.vmap(lambda k: jax.random.permutation(k, SLOTS))(jax.random.split(k_order, N_TILES)).astype(jnp.int32)
    taken = jnp.arange(SLOTS, dtype=jnp.int32)[None, :] < counts[:, None]
    slot_of = (orders + jnp.arange(N_TILES, dtype=jnp.int32)[:, None] * SLOTS).reshape(-1).astype(jnp.int32)
    live_order = taken.reshape(-1)
    position = jnp.arange(SLOTS_ALL, dtype=jnp.int32)
    before = lax.cummax(jnp.where(live_order, position, -1), axis=0)
    prev = jnp.concatenate([jnp.array([-1], dtype=jnp.int32), before[:-1]])
    after = lax.cummin(jnp.where(live_order, position, SLOTS_ALL), axis=0, reverse=True)
    nxt = jnp.concatenate([after[1:], jnp.array([SLOTS_ALL], dtype=jnp.int32)])
    upper = jnp.where(live_order & (prev >= 0), slot_of[jnp.clip(prev, 0, SLOTS_ALL - 1)], -1)
    lower = jnp.where(live_order & (nxt < SLOTS_ALL), slot_of[jnp.clip(nxt, 0, SLOTS_ALL - 1)], -1)
    live = jnp.zeros((SLOTS_ALL,), jnp.int32).at[slot_of].set(live_order.astype(jnp.int32))
    pairs = jnp.stack([upper, lower], axis=1).astype(jnp.int32)
    neigh = jnp.full((SLOTS_ALL, 2), -1, jnp.int32).at[slot_of].set(pairs)
    return (live, neigh)


def draw_live(key, part):
    return build_chain(key)[0]


def draw_neighbours(key, part):
    return build_chain(key)[1]


def draw_coarse_perm(key, part):
    keys = jax.random.split(jax.random.fold_in(key, 23), N_TILES)
    return jax.vmap(lambda k: jax.random.permutation(k, SLOTS))(keys).astype(jnp.int32)


def block_levels(stream_key, shape, pieces, smallest, high):
    def one(axis_at, parts):
        heights = jax.random.uniform(jax.random.fold_in(jax.random.fold_in(stream_key, 6), axis_at), (parts,), jnp.float32, smallest / len(pieces), high / len(pieces))
        return jnp.repeat(jnp.exp(heights), shape[axis_at] // parts).reshape((-1,) + (1,) * (len(shape) - axis_at - 1))

    level = one(*pieces[0])
    for cut in pieces[1:]:
        level = level * one(*cut)
    return level


def normal_values(rng, shape, deviation, reach, cuts=(), kind=jnp.bfloat16):
    entries = deviation * jax.random.normal(rng, shape, jnp.float32)
    if cuts:
        entries = entries * block_levels(rng, shape, cuts, -0.22, 0.18)
    return jnp.clip(entries, -reach, reach).astype(kind)


def setup_inputs(seed: int = 0, part: int = 0) -> dict:
    arg_keys = jax.random.split(jax.random.key(seed), 16)
    part_keys = jax.random.split(jax.random.fold_in(arg_keys[15], part), 16)
    return {
        "features": normal_values(part_keys[0], (BANDS, SLOTS_ALL, XC, TR, W), 1.0, 6.0, ((0, 2), (1, 4))),
        "state": normal_values(part_keys[1], (BANDS, SLOTS_ALL, C, TR, W), 0.5, 3.0, ((0, 2), (1, 4)), jnp.float32),
        "live": draw_live(jax.random.fold_in(arg_keys[15], 71), part),
        "neighbours": draw_neighbours(jax.random.fold_in(arg_keys[15], 71), part),
        "coarse_perm": draw_coarse_perm(jax.random.fold_in(arg_keys[15], 71), part),
        "coarse_state": normal_values(part_keys[5], (SLOTS_ALL, C, CR, CW), 0.5, 3.0, ((0, 8),), jnp.float32),
        "w_update": normal_values(arg_keys[6], (9, C, C + XC), (9 * (C + XC)) ** -0.5, 0.5),
        "b_update": normal_values(arg_keys[7], (C,), 0.5, 3.0, (), jnp.float32),
        "w_reset": normal_values(arg_keys[8], (9, C, C + XC), (9 * (C + XC)) ** -0.5, 0.5),
        "b_reset": normal_values(arg_keys[9], (C,), 0.5, 3.0, (), jnp.float32),
        "w_cand": normal_values(arg_keys[10], (9, C, C + XC), (9 * (C + XC)) ** -0.5, 0.5),
        "b_cand": normal_values(arg_keys[11], (C,), 0.5, 3.0, (), jnp.float32),
        "u_pool": normal_values(arg_keys[12], (C, C), C ** -0.5, 1.5, (), jnp.float32),
        "u_state": normal_values(arg_keys[13], (C, C), C ** -0.5, 1.5, (), jnp.float32),
        "b_coarse": normal_values(arg_keys[14], (C,), 0.5, 3.0, (), jnp.float32),
    }


def pad_slots(arr, nbr, depth):
    row_count = arr.shape[2]
    ups = nbr[:, 0]
    downs = nbr[:, 1]
    top = jnp.take(arr[:, :, row_count - depth:, :], jnp.clip(ups, 0, arr.shape[0] - 1), axis=0)
    top = jnp.where((ups >= 0)[:, None, None, None], top, jnp.zeros_like(top))
    bottom = jnp.take(arr[:, :, :depth, :], jnp.clip(downs, 0, arr.shape[0] - 1), axis=0)
    bottom = jnp.where((downs >= 0)[:, None, None, None], bottom, jnp.zeros_like(bottom))
    full = jnp.concatenate([top, arr, bottom], axis=2)
    return jnp.pad(full, ((0, 0), (0, 0), (0, 0), (2, 2)))


def apply_filter(padded_input, filter_weight, dilation_rate, row_count, column_count):
    total = jnp.zeros((padded_input.shape[0], filter_weight.shape[1], row_count, column_count), jnp.float32)
    for left_operand in (-1, 0, 1):
        for right_operand in (-1, 0, 1):
            window_slice = padded_input[:, :, 2 + left_operand * dilation_rate:2 + left_operand * dilation_rate + row_count, 2 + right_operand * dilation_rate:2 + right_operand * dilation_rate + column_count]
            weight = filter_weight[(left_operand + 1) * 3 + (right_operand + 1)].astype(jnp.float32)
            total = total + jnp.einsum('oi,sirw->sorw', weight, window_slice.astype(jnp.float32))
    return total


def reference(features, state, live, neighbours, coarse_perm, coarse_state, w_update, b_update, w_reset, b_reset, w_cand, b_cand, u_pool, u_state, b_coarse):
    row_count = state.shape[3]
    column_count = state.shape[4]
    alive = live.astype(jnp.float32)[:, None, None, None]

    def one_band(pair):
        feats, hidden = pair
        hb = hidden.astype(jnp.bfloat16)
        joined = jnp.concatenate([feats, hb], axis=1)
        first = pad_slots(joined, neighbours, 2)
        update = jax.nn.sigmoid(apply_filter(first, w_update, 1, row_count, column_count) + b_update[:, None, None])
        reset = jax.nn.sigmoid(apply_filter(first, w_reset, 1, row_count, column_count) + b_reset[:, None, None])
        gated = (reset * hb.astype(jnp.float32)).astype(jnp.bfloat16)
        second = pad_slots(jnp.concatenate([feats, gated], axis=1), neighbours, 2)
        candidate = jnp.tanh(apply_filter(second, w_cand, 2, row_count, column_count) + b_cand[:, None, None])
        return ((1.0 - update) * hidden + update * candidate) * alive

    new_state = lax.map(one_band, (features, state))
    slots = state.shape[1]
    chans = state.shape[2]
    summed = jnp.sum(new_state, axis=0)
    pooled = summed.reshape(slots, chans, row_count // 4, 4, column_count // 4, 4).sum(axis=(3, 5)) / 16.0
    tiles_count = coarse_perm.shape[0]
    per = coarse_perm.shape[1]
    source = (jnp.arange(tiles_count, dtype=jnp.int32)[:, None] * per + coarse_perm).reshape(-1).astype(jnp.int32)
    picked = jnp.take(pooled, source, axis=0)
    pre = jnp.einsum('oc,kcij->koij', u_pool, picked, precision=lax.Precision.HIGHEST)
    pre = pre + jnp.einsum('oc,kcij->koij', u_state, coarse_state, precision=lax.Precision.HIGHEST)
    pre = pre + b_coarse[None, :, None, None]
    coarse_next = coarse_state + jnp.tanh(pre)
    return new_state, coarse_next
```

```python
import jax
import jax.numpy as jnp
from jax import lax
from jax.sharding import PartitionSpec as P


def padded(block, sides, width):
    for axis, dim in sides:
        count = lax.axis_size(axis)
        forward = [(i, i + 1) for i in range(count - 1)]
        backward = [(target, source) for source, target in forward]
        low = lax.ppermute(
            lax.slice_in_dim(block, block.shape[dim] - width, None, axis=dim), axis, forward
        )
        high = lax.ppermute(lax.slice_in_dim(block, 0, width, axis=dim), axis, backward)
        block = jnp.concatenate([low, block, high], axis=dim)
    return block


def apply_filter(
    padded_input, filter_weight, dilation_rate, first_row_index, row_count, column_count
):
    total = None
    for left_operand in (-1, 0, 1):
        for right_operand in (-1, 0, 1):
            window_slice = padded_input[
                :,
                :,
                :,
                first_row_index
                + left_operand * dilation_rate : first_row_index
                + left_operand * dilation_rate
                + row_count,
                2
                + right_operand * dilation_rate : 2
                + right_operand * dilation_rate
                + column_count,
            ]
            term = jnp.einsum(
                "oi,bsirw->bsorw",
                filter_weight[(left_operand + 1) * 3 + (right_operand + 1)],
                window_slice,
                preferred_element_type=jnp.float32,
            )
            total = term if total is None else total + term
    return total


def choose_rows(block, select):
    masked = jnp.where(select[None, :, None, None, None], block, jnp.zeros_like(block))
    return jnp.sum(masked, axis=1)


def exchange_sum(part, owned):
    bands = lax.axis_size("band")
    reps = lax.axis_size("rep")
    band = lax.axis_index("band")
    total = None
    for shift in range(bands):
        pair = None
        for step in range(reps):
            target = (band + shift) % bands
            chunk = lax.dynamic_slice_in_dim(part, target * owned, owned, 0)
            if shift or step:
                perm = [
                    (b * reps + r, ((b + shift) % bands) * reps + (r + step) % reps)
                    for b in range(bands)
                    for r in range(reps)
                ]
                chunk = lax.ppermute(chunk, ("band", "rep"), perm)
            pair = chunk if pair is None else pair + chunk
        total = pair if total is None else total + pair
    return total


def shards(
    features,
    state,
    live,
    neighbours,
    coarse_perm,
    coarse_state,
    w_update,
    b_update,
    w_reset,
    b_reset,
    w_cand,
    b_cand,
    u_pool,
    u_state,
    b_coarse,
):
    slots = state.shape[1]
    chans = state.shape[2]
    row_count = state.shape[3]
    column_count = state.shape[4]
    inputs_count = features.shape[2]
    half = chans // lax.axis_size("rep")
    start = lax.axis_index("rep") * half
    base = lax.axis_index("tiles") * slots
    ups = neighbours[:, 0]
    downs = neighbours[:, 1]
    up_here = (ups >= base) & (ups < base + slots)
    down_here = (downs >= base) & (downs < base + slots)
    up_far = (ups >= 0) & jnp.logical_not(up_here)
    down_far = (downs >= 0) & jnp.logical_not(down_here)
    alive = live > 0
    first_sel = alive & jnp.logical_not(up_here)
    last_sel = alive & jnp.logical_not(down_here)

    def own_out(filter_weight):
        return lax.dynamic_slice_in_dim(filter_weight, start, half, 1)

    def own_bias(bias):
        return lax.dynamic_slice_in_dim(bias, start, half, 0)[:, None, None]

    hb = state.astype(jnp.bfloat16)
    joined = jnp.concatenate([features, hb], axis=2)
    top = choose_rows(joined[:, :, :, :3, :], first_sel)
    bottom = choose_rows(joined[:, :, :, row_count - 3 :, :], last_sel)
    cycle = padded(jnp.concatenate([top, bottom], axis=2), (("tiles", 2),), 3)
    cycle_prev = cycle[:, None, :, :3, :]
    cycle_next = cycle[:, None, :, 3 * 3 : 4 * 3, :]
    top_local = jnp.take(
        joined[:, :, :, row_count - 3 :, :], jnp.clip(ups - base, 0, slots - 1), axis=1
    )
    bottom_local = jnp.take(joined[:, :, :, :3, :], jnp.clip(downs - base, 0, slots - 1), axis=1)
    zeros_rows = jnp.zeros_like(top_local)
    top = jnp.where(
        up_here[None, :, None, None, None],
        top_local,
        jnp.where(up_far[None, :, None, None, None], cycle_prev + zeros_rows, zeros_rows),
    )
    bottom = jnp.where(
        down_here[None, :, None, None, None],
        bottom_local,
        jnp.where(down_far[None, :, None, None, None], cycle_next + zeros_rows, zeros_rows),
    )
    full = jnp.concatenate([top, joined, bottom], axis=3)
    first = jnp.pad(full, ((0, 0), (0, 0), (0, 0), (0, 0), (2, 2)))
    update = jax.nn.sigmoid(
        apply_filter(first, own_out(w_update), 1, 3, row_count, column_count) + own_bias(b_update)
    )
    hidden_wide = first[:, :, inputs_count:, 1 : row_count + 5, 2 : column_count + 2]
    reset_half = jax.nn.sigmoid(
        apply_filter(first, own_out(w_reset), 1, 1, row_count + 4, column_count) + own_bias(b_reset)
    )
    wide_half = lax.dynamic_slice_in_dim(hidden_wide, start, half, 2)
    gated = lax.all_gather(
        (reset_half * wide_half.astype(jnp.float32)).astype(jnp.bfloat16), "rep", axis=2, tiled=True
    )
    gated_pad = jnp.pad(gated, ((0, 0), (0, 0), (0, 0), (0, 0), (2, 2)))
    second = jnp.concatenate([first[:, :, :inputs_count, 1 : row_count + 5, :], gated_pad], axis=2)
    candidate = jnp.tanh(
        apply_filter(second, own_out(w_cand), 2, 2, row_count, column_count) + own_bias(b_cand)
    )
    state_half = lax.dynamic_slice_in_dim(state, start, half, 2)
    live_scale = alive.astype(jnp.float32)[None, :, None, None, None]
    new_half = ((1.0 - update) * state_half + update * candidate) * live_scale
    band_local = new_half.shape[0]
    blocks = new_half.reshape(band_local, slots, half, row_count // 4, 4, column_count // 4, 4)
    pooled = jnp.sum(jnp.sum(blocks, axis=(4, 6)), axis=0) / 16.0
    ordered = jnp.take(pooled, coarse_perm[0], axis=0)
    part = jnp.einsum(
        "oc,kcij->koij",
        lax.dynamic_slice_in_dim(u_pool, start, half, 1),
        ordered,
        precision=lax.Precision.HIGHEST,
    )
    pre = exchange_sum(part, coarse_state.shape[0])
    pre = pre + jnp.einsum("oc,kcij->koij", u_state, coarse_state, precision=lax.Precision.HIGHEST)
    pre = pre + b_coarse[None, :, None, None]
    coarse_next = coarse_state + jnp.tanh(pre)
    return (new_half, coarse_next)


def solution(mesh):
    return jax.shard_map(
        shards,
        mesh=mesh,
        in_specs=(
            P(("groups", "band"), "tiles", None, None, None),
            P(("groups", "band"), "tiles", None, None, None),
            P("tiles"),
            P("tiles", None),
            P("tiles", None),
            P(("groups", "tiles", "band"), None, None, None),
            P(),
            P(),
            P(),
            P(),
            P(),
            P(),
            P(),
            P(),
            P(),
        ),
        out_specs=(
            P(("groups", "band"), "tiles", "rep", None, None),
            P(("groups", "tiles", "band"), None, None, None),
        ),
        check_vma=False,
    )
```

```python
import jax
import jax.numpy as jnp
from jax import lax
from jax.sharding import PartitionSpec as P


def padded(block, sides, width):
    for axis, dim in sides:
        count = lax.axis_size(axis)
        forward = [(i, i + 1) for i in range(count - 1)]
        backward = [(target, source) for source, target in forward]
        low = lax.ppermute(
            lax.slice_in_dim(block, block.shape[dim] - width, None, axis=dim), axis, forward
        )
        high = lax.ppermute(lax.slice_in_dim(block, 0, width, axis=dim), axis, backward)
        block = jnp.concatenate([low, block, high], axis=dim)
    return block


def apply_filter(
    padded_input, filter_weight, dilation_rate, first_row_index, row_count, column_count
):
    total = None
    for left_operand in (-1, 0, 1):
        for right_operand in (-1, 0, 1):
            window_slice = padded_input[
                :,
                :,
                :,
                first_row_index
                + left_operand * dilation_rate : first_row_index
                + left_operand * dilation_rate
                + row_count,
                2
                + right_operand * dilation_rate : 2
                + right_operand * dilation_rate
                + column_count,
            ]
            term = jnp.einsum(
                "oi,bsirw->bsorw",
                filter_weight[(left_operand + 1) * 3 + (right_operand + 1)],
                window_slice,
                preferred_element_type=jnp.float32,
            )
            total = term if total is None else total + term
    return total


def choose_rows(block, select):
    masked = jnp.where(select[None, :, None, None, None], block, jnp.zeros_like(block))
    return jnp.sum(masked, axis=1)


def exchange_sum(part, owned):
    bands = lax.axis_size("band")
    reps = lax.axis_size("rep")
    band = lax.axis_index("band")
    total = None
    for shift in range(bands):
        pair = None
        for step in range(reps):
            target = (band + shift) % bands
            chunk = lax.dynamic_slice_in_dim(part, target * owned, owned, 0)
            if shift or step:
                perm = [
                    (b * reps + r, ((b + shift) % bands) * reps + (r + step) % reps)
                    for b in range(bands)
                    for r in range(reps)
                ]
                chunk = lax.ppermute(chunk, ("band", "rep"), perm)
            pair = chunk if pair is None else pair + chunk
        total = pair if total is None else total + pair
    return total


def shards(
    features,
    state,
    live,
    neighbours,
    coarse_perm,
    coarse_state,
    w_update,
    b_update,
    w_reset,
    b_reset,
    w_cand,
    b_cand,
    u_pool,
    u_state,
    b_coarse,
):
    slots = state.shape[1]
    chans = state.shape[2]
    row_count = state.shape[3]
    column_count = state.shape[4]
    inputs_count = features.shape[2]
    half = chans // lax.axis_size("rep")
    start = lax.axis_index("rep") * half
    base = lax.axis_index("tiles") * slots
    ups = neighbours[:, 0]
    downs = neighbours[:, 1]
    up_here = (ups >= base) & (ups < base + slots)
    down_here = (downs >= base) & (downs < base + slots)
    up_far = (ups >= 0) & jnp.logical_not(up_here)
    down_far = (downs >= 0) & jnp.logical_not(down_here)
    alive = live > 0
    first_sel = alive & jnp.logical_not(up_here)
    last_sel = alive & jnp.logical_not(down_here)

    def own_out(filter_weight):
        return lax.dynamic_slice_in_dim(filter_weight, start, half, 1)

    def own_bias(bias):
        return lax.dynamic_slice_in_dim(bias, start, half, 0)[:, None, None]

    hb = state.astype(jnp.bfloat16)
    joined = jnp.concatenate([features, hb], axis=2)
    top = choose_rows(joined[:, :, :, :3, :], first_sel)
    bottom = choose_rows(joined[:, :, :, row_count - 3 :, :], last_sel)
    cycle = padded(jnp.concatenate([top, bottom], axis=2), (("tiles", 2),), 3)
    cycle_prev = cycle[:, None, :, :3, :]
    cycle_next = cycle[:, None, :, 3 * 3 : 4 * 3, :]
    top_local = jnp.take(
        joined[:, :, :, row_count - 3 :, :], jnp.clip(ups - base, 0, slots - 1), axis=1
    )
    bottom_local = jnp.take(joined[:, :, :, :3, :], jnp.clip(downs - base, 0, slots - 1), axis=1)
    zeros_rows = jnp.zeros_like(top_local)
    top = jnp.where(
        up_here[None, :, None, None, None],
        top_local,
        jnp.where(up_far[None, :, None, None, None], cycle_prev + zeros_rows, zeros_rows),
    )
    bottom = jnp.where(
        down_here[None, :, None, None, None],
        bottom_local,
        jnp.where(down_far[None, :, None, None, None], cycle_next + zeros_rows, zeros_rows),
    )
    full = jnp.concatenate([top, joined, bottom], axis=3)
    first = jnp.pad(full, ((0, 0), (0, 0), (0, 0), (0, 0), (2, 2)))
    update = jax.nn.sigmoid(
        apply_filter(first, own_out(w_update), 1, 3, row_count, column_count) + own_bias(b_update)
    )
    hidden_wide = first[:, :, inputs_count:, 1 : row_count + 5, 2 : column_count + 2]
    reset_half = jax.nn.sigmoid(
        apply_filter(first, own_out(w_reset), 1, 1, row_count + 4, column_count) + own_bias(b_reset)
    )
    wide_half = lax.dynamic_slice_in_dim(hidden_wide, start, half, 2)
    gated = lax.all_gather(
        (reset_half * wide_half.astype(jnp.float32)).astype(jnp.bfloat16), "rep", axis=2, tiled=True
    )
    gated_pad = jnp.pad(gated, ((0, 0), (0, 0), (0, 0), (0, 0), (2, 2)))
    second = jnp.concatenate([first[:, :, :inputs_count, 1 : row_count + 5, :], gated_pad], axis=2)
    candidate = jnp.tanh(
        apply_filter(second, own_out(w_cand), 2, 2, row_count, column_count) + own_bias(b_cand)
    )
    state_half = lax.dynamic_slice_in_dim(state, start, half, 2)
    live_scale = alive.astype(jnp.float32)[None, :, None, None, None]
    new_half = ((1.0 - update) * state_half + update * candidate) * live_scale
    summed = jnp.sum(new_half, axis=0)
    column_pool = (
        jnp.arange(column_count)[:, None] // 4 == jnp.arange(column_count // 4)[None, :]
    ).astype(jnp.float32)
    cols = jnp.einsum(
        "schw,wj->schj", summed, column_pool, precision=lax.Precision.HIGHEST
    )
    pooled = jnp.sum(
        cols.reshape(slots, half, row_count // 4, 4, column_count // 4), axis=3
    ) / 16.0
    ordered = jnp.take(pooled, coarse_perm[0], axis=0)
    part = jnp.einsum(
        "oc,kcij->koij",
        lax.dynamic_slice_in_dim(u_pool, start, half, 1),
        ordered,
        precision=lax.Precision.HIGHEST,
    )
    pre = exchange_sum(part, coarse_state.shape[0])
    pre = pre + jnp.einsum("oc,kcij->koij", u_state, coarse_state, precision=lax.Precision.HIGHEST)
    pre = pre + b_coarse[None, :, None, None]
    coarse_next = coarse_state + jnp.tanh(pre)
    return (new_half, coarse_next)


def solution(mesh):
    return jax.shard_map(
        shards,
        mesh=mesh,
        in_specs=(
            P(("groups", "band"), "tiles", None, None, None),
            P(("groups", "band"), "tiles", None, None, None),
            P("tiles"),
            P("tiles", None),
            P("tiles", None),
            P(("groups", "tiles", "band"), None, None, None),
            P(),
            P(),
            P(),
            P(),
            P(),
            P(),
            P(),
            P(),
            P(),
        ),
        out_specs=(
            P(("groups", "band"), "tiles", "rep", None, None),
            P(("groups", "tiles", "band"), None, None, None),
        ),
        check_vma=False,
    )
```

```python
import jax
import jax.numpy as jnp
from jax import lax
from jax.sharding import PartitionSpec as P


def padded(block, sides, width):
    for axis, dim in sides:
        count = lax.axis_size(axis)
        forward = [(i, i + 1) for i in range(count - 1)]
        backward = [(target, source) for source, target in forward]
        low = lax.ppermute(
            lax.slice_in_dim(block, block.shape[dim] - width, None, axis=dim), axis, forward
        )
        high = lax.ppermute(lax.slice_in_dim(block, 0, width, axis=dim), axis, backward)
        block = jnp.concatenate([low, block, high], axis=dim)
    return block


def apply_filter(
    padded_input, filter_weight, dilation_rate, first_row_index, row_count, column_count
):
    total = None
    for left_operand in (-1, 0, 1):
        for right_operand in (-1, 0, 1):
            window_slice = padded_input[
                :,
                :,
                :,
                first_row_index
                + left_operand * dilation_rate : first_row_index
                + left_operand * dilation_rate
                + row_count,
                2
                + right_operand * dilation_rate : 2
                + right_operand * dilation_rate
                + column_count,
            ]
            term = jnp.einsum(
                "oi,bsirw->bsorw",
                filter_weight[(left_operand + 1) * 3 + (right_operand + 1)],
                window_slice,
                preferred_element_type=jnp.float32,
            )
            total = term if total is None else total + term
    return total


def choose_rows(block, select):
    masked = jnp.where(select[None, :, None, None, None], block, jnp.zeros_like(block))
    return jnp.sum(masked, axis=1)


def exchange_sum(part, owned):
    bands = lax.axis_size("band")
    reps = lax.axis_size("rep")
    band = lax.axis_index("band")
    total = None
    for shift in range(bands):
        pair = None
        for step in range(reps):
            target = (band + shift) % bands
            chunk = lax.dynamic_slice_in_dim(part, target * owned, owned, 0)
            if shift or step:
                perm = [
                    (b * reps + r, ((b + shift) % bands) * reps + (r + step) % reps)
                    for b in range(bands)
                    for r in range(reps)
                ]
                chunk = lax.ppermute(chunk, ("band", "rep"), perm)
            pair = chunk if pair is None else pair + chunk
        total = pair if total is None else total + pair
    return total


def shards(
    features,
    state,
    live,
    neighbours,
    coarse_perm,
    coarse_state,
    w_update,
    b_update,
    w_reset,
    b_reset,
    w_cand,
    b_cand,
    u_pool,
    u_state,
    b_coarse,
):
    slots = state.shape[1]
    chans = state.shape[2]
    row_count = state.shape[3]
    column_count = state.shape[4]
    inputs_count = features.shape[2]
    half = chans // lax.axis_size("rep")
    start = lax.axis_index("rep") * half
    base = lax.axis_index("tiles") * slots
    ups = neighbours[:, 0]
    downs = neighbours[:, 1]
    up_here = (ups >= base) & (ups < base + slots)
    down_here = (downs >= base) & (downs < base + slots)
    up_far = (ups >= 0) & jnp.logical_not(up_here)
    down_far = (downs >= 0) & jnp.logical_not(down_here)
    alive = live > 0
    first_sel = alive & jnp.logical_not(up_here)
    last_sel = alive & jnp.logical_not(down_here)

    def own_out(filter_weight):
        return lax.dynamic_slice_in_dim(filter_weight, start, half, 1)

    def own_bias(bias):
        return lax.dynamic_slice_in_dim(bias, start, half, 0)[:, None, None]

    hb = state.astype(jnp.bfloat16)
    joined = jnp.concatenate([features, hb], axis=2)
    top = choose_rows(joined[:, :, :, :3, :], first_sel)
    bottom = choose_rows(joined[:, :, :, row_count - 3 :, :], last_sel)
    cycle = padded(jnp.concatenate([top, bottom], axis=2), (("tiles", 2),), 3)
    cycle_prev = cycle[:, None, :, :3, :]
    cycle_next = cycle[:, None, :, 3 * 3 : 4 * 3, :]
    top_local = jnp.take(
        joined[:, :, :, row_count - 3 :, :], jnp.clip(ups - base, 0, slots - 1), axis=1
    )
    bottom_local = jnp.take(joined[:, :, :, :3, :], jnp.clip(downs - base, 0, slots - 1), axis=1)
    zeros_rows = jnp.zeros_like(top_local)
    top = jnp.where(
        up_here[None, :, None, None, None],
        top_local,
        jnp.where(up_far[None, :, None, None, None], cycle_prev + zeros_rows, zeros_rows),
    )
    bottom = jnp.where(
        down_here[None, :, None, None, None],
        bottom_local,
        jnp.where(down_far[None, :, None, None, None], cycle_next + zeros_rows, zeros_rows),
    )
    full = jnp.concatenate([top, joined, bottom], axis=3)
    first = jnp.pad(full, ((0, 0), (0, 0), (0, 0), (0, 0), (2, 2)))
    update = jax.nn.sigmoid(
        apply_filter(first, own_out(w_update), 1, 3, row_count, column_count) + own_bias(b_update)
    )
    hidden_wide = first[:, :, inputs_count:, 1 : row_count + 5, 2 : column_count + 2]
    reset_half = jax.nn.sigmoid(
        apply_filter(first, own_out(w_reset), 1, 1, row_count + 4, column_count) + own_bias(b_reset)
    )
    wide_half = lax.dynamic_slice_in_dim(hidden_wide, start, half, 2)
    gated_half = (reset_half * wide_half.astype(jnp.float32)).astype(jnp.bfloat16)
    reps = lax.axis_size("rep")
    pieces = [gated_half]
    for step in range(1, reps):
        perm = [(r, (r + step) % reps) for r in range(reps)]
        pieces.append(lax.ppermute(gated_half, "rep", perm))
    rep = lax.axis_index("rep")
    gated = jnp.concatenate(
        [
            sum(
                jnp.where((rep - step) % reps == owner, piece, jnp.zeros_like(piece))
                for step, piece in enumerate(pieces)
            )
            for owner in range(reps)
        ],
        axis=2,
    )
    gated_pad = jnp.pad(gated, ((0, 0), (0, 0), (0, 0), (0, 0), (2, 2)))
    second = jnp.concatenate([first[:, :, :inputs_count, 1 : row_count + 5, :], gated_pad], axis=2)
    candidate = jnp.tanh(
        apply_filter(second, own_out(w_cand), 2, 2, row_count, column_count) + own_bias(b_cand)
    )
    state_half = lax.dynamic_slice_in_dim(state, start, half, 2)
    live_scale = alive.astype(jnp.float32)[None, :, None, None, None]
    new_half = ((1.0 - update) * state_half + update * candidate) * live_scale
    summed = jnp.sum(new_half, axis=0)
    column_pool = (
        jnp.arange(column_count)[:, None] // 4 == jnp.arange(column_count // 4)[None, :]
    ).astype(jnp.float32)
    cols = jnp.einsum(
        "schw,wj->schj", summed, column_pool, precision=lax.Precision.HIGHEST
    )
    pooled = jnp.sum(
        cols.reshape(slots, half, row_count // 4, 4, column_count // 4), axis=3
    ) / 16.0
    ordered = jnp.take(pooled, coarse_perm[0], axis=0)
    part = jnp.einsum(
        "oc,kcij->koij",
        lax.dynamic_slice_in_dim(u_pool, start, half, 1),
        ordered,
        precision=lax.Precision.HIGHEST,
    )
    pre = exchange_sum(part, coarse_state.shape[0])
    pre = pre + jnp.einsum("oc,kcij->koij", u_state, coarse_state, precision=lax.Precision.HIGHEST)
    pre = pre + b_coarse[None, :, None, None]
    coarse_next = coarse_state + jnp.tanh(pre)
    return (new_half, coarse_next)


def solution(mesh):
    return jax.shard_map(
        shards,
        mesh=mesh,
        in_specs=(
            P(("groups", "band"), "tiles", None, None, None),
            P(("groups", "band"), "tiles", None, None, None),
            P("tiles"),
            P("tiles", None),
            P("tiles", None),
            P(("groups", "tiles", "band"), None, None, None),
            P(),
            P(),
            P(),
            P(),
            P(),
            P(),
            P(),
            P(),
            P(),
        ),
        out_specs=(
            P(("groups", "band"), "tiles", "rep", None, None),
            P(("groups", "tiles", "band"), None, None, None),
        ),
        check_vma=False,
    )
```

```python
import jax
import jax.numpy as jnp
from jax import lax
from jax.sharding import PartitionSpec as P


def padded(block, sides, width):
    for axis, dim in sides:
        count = lax.axis_size(axis)
        forward = [(i, i + 1) for i in range(count - 1)]
        backward = [(target, source) for source, target in forward]
        low = lax.ppermute(
            lax.slice_in_dim(block, block.shape[dim] - width, None, axis=dim), axis, forward
        )
        high = lax.ppermute(lax.slice_in_dim(block, 0, width, axis=dim), axis, backward)
        block = jnp.concatenate([low, block, high], axis=dim)
    return block


def apply_filter(
    padded_input, filter_weight, dilation_rate, first_row_index, row_count, column_count
):
    total = None
    for left_operand in (-1, 0, 1):
        for right_operand in (-1, 0, 1):
            window_slice = padded_input[
                :,
                :,
                :,
                first_row_index
                + left_operand * dilation_rate : first_row_index
                + left_operand * dilation_rate
                + row_count,
                2
                + right_operand * dilation_rate : 2
                + right_operand * dilation_rate
                + column_count,
            ]
            term = jnp.einsum(
                "oi,bsirw->bsorw",
                filter_weight[(left_operand + 1) * 3 + (right_operand + 1)],
                window_slice,
                preferred_element_type=jnp.float32,
            )
            total = term if total is None else total + term
    return total


def choose_rows(block, select):
    masked = jnp.where(select[None, :, None, None, None], block, jnp.zeros_like(block))
    return jnp.sum(masked, axis=1)


def exchange_sum(part, owned):
    bands = lax.axis_size("band")
    reps = lax.axis_size("rep")
    band = lax.axis_index("band")
    total = None
    for shift in range(bands):
        pair = None
        for step in range(reps):
            target = (band + shift) % bands
            chunk = lax.dynamic_slice_in_dim(part, target * owned, owned, 0)
            if shift or step:
                perm = [
                    (b * reps + r, ((b + shift) % bands) * reps + (r + step) % reps)
                    for b in range(bands)
                    for r in range(reps)
                ]
                chunk = lax.ppermute(chunk, ("band", "rep"), perm)
            pair = chunk if pair is None else pair + chunk
        total = pair if total is None else total + pair
    return total


def shards(
    features,
    state,
    live,
    neighbours,
    coarse_perm,
    coarse_state,
    w_update,
    b_update,
    w_reset,
    b_reset,
    w_cand,
    b_cand,
    u_pool,
    u_state,
    b_coarse,
):
    slots = state.shape[1]
    chans = state.shape[2]
    row_count = state.shape[3]
    column_count = state.shape[4]
    inputs_count = features.shape[2]
    half = chans // lax.axis_size("rep")
    start = lax.axis_index("rep") * half
    base = lax.axis_index("tiles") * slots
    ups = neighbours[:, 0]
    downs = neighbours[:, 1]
    up_here = (ups >= base) & (ups < base + slots)
    down_here = (downs >= base) & (downs < base + slots)
    up_far = (ups >= 0) & jnp.logical_not(up_here)
    down_far = (downs >= 0) & jnp.logical_not(down_here)
    alive = live > 0
    first_sel = alive & jnp.logical_not(up_here)
    last_sel = alive & jnp.logical_not(down_here)

    def own_out(filter_weight):
        return lax.dynamic_slice_in_dim(filter_weight, start, half, 1)

    def own_bias(bias):
        return lax.dynamic_slice_in_dim(bias, start, half, 0)[:, None, None]

    hb = state.astype(jnp.bfloat16)
    joined = jnp.concatenate([features, hb], axis=2)
    top = choose_rows(joined[:, :, :, :3, :], first_sel)
    bottom = choose_rows(joined[:, :, :, row_count - 3 :, :], last_sel)
    tiles_count = lax.axis_size("tiles")
    tile = lax.axis_index("tiles")
    edges = lax.all_gather(jnp.concatenate([top, bottom], axis=2), "tiles")
    cycle_prev = lax.dynamic_index_in_dim(edges, (tile + tiles_count - 1) % tiles_count, 0, False)
    cycle_next = lax.dynamic_index_in_dim(edges, (tile + 1) % tiles_count, 0, False)
    cycle_prev = cycle_prev[:, None, :, 3:6, :]
    cycle_next = cycle_next[:, None, :, :3, :]
    top_local = jnp.take(
        joined[:, :, :, row_count - 3 :, :], jnp.clip(ups - base, 0, slots - 1), axis=1
    )
    bottom_local = jnp.take(joined[:, :, :, :3, :], jnp.clip(downs - base, 0, slots - 1), axis=1)
    zeros_rows = jnp.zeros_like(top_local)
    top = jnp.where(
        up_here[None, :, None, None, None],
        top_local,
        jnp.where(up_far[None, :, None, None, None], cycle_prev + zeros_rows, zeros_rows),
    )
    bottom = jnp.where(
        down_here[None, :, None, None, None],
        bottom_local,
        jnp.where(down_far[None, :, None, None, None], cycle_next + zeros_rows, zeros_rows),
    )
    full = jnp.concatenate([top, joined, bottom], axis=3)
    first = jnp.pad(full, ((0, 0), (0, 0), (0, 0), (0, 0), (2, 2)))
    update = jax.nn.sigmoid(
        apply_filter(first, own_out(w_update), 1, 3, row_count, column_count) + own_bias(b_update)
    )
    hidden_wide = first[:, :, inputs_count:, 1 : row_count + 5, 2 : column_count + 2]
    reset_half = jax.nn.sigmoid(
        apply_filter(first, own_out(w_reset), 1, 1, row_count + 4, column_count) + own_bias(b_reset)
    )
    wide_half = lax.dynamic_slice_in_dim(hidden_wide, start, half, 2)
    gated = lax.all_gather(
        (reset_half * wide_half.astype(jnp.float32)).astype(jnp.bfloat16), "rep", axis=2, tiled=True
    )
    gated_pad = jnp.pad(gated, ((0, 0), (0, 0), (0, 0), (0, 0), (2, 2)))
    second = jnp.concatenate([first[:, :, :inputs_count, 1 : row_count + 5, :], gated_pad], axis=2)
    candidate = jnp.tanh(
        apply_filter(second, own_out(w_cand), 2, 2, row_count, column_count) + own_bias(b_cand)
    )
    state_half = lax.dynamic_slice_in_dim(state, start, half, 2)
    live_scale = alive.astype(jnp.float32)[None, :, None, None, None]
    new_half = ((1.0 - update) * state_half + update * candidate) * live_scale
    summed = jnp.sum(new_half, axis=0)
    column_pool = (
        jnp.arange(column_count)[:, None] // 4 == jnp.arange(column_count // 4)[None, :]
    ).astype(jnp.float32)
    cols = jnp.einsum(
        "schw,wj->schj", summed, column_pool, precision=lax.Precision.HIGHEST
    )
    pooled = jnp.sum(
        cols.reshape(slots, half, row_count // 4, 4, column_count // 4), axis=3
    ) / 16.0
    ordered = jnp.take(pooled, coarse_perm[0], axis=0)
    part = jnp.einsum(
        "oc,kcij->koij",
        lax.dynamic_slice_in_dim(u_pool, start, half, 1),
        ordered,
        precision=lax.Precision.HIGHEST,
    )
    pre = exchange_sum(part, coarse_state.shape[0])
    pre = pre + jnp.einsum("oc,kcij->koij", u_state, coarse_state, precision=lax.Precision.HIGHEST)
    pre = pre + b_coarse[None, :, None, None]
    coarse_next = coarse_state + jnp.tanh(pre)
    return (new_half, coarse_next)


def solution(mesh):
    return jax.shard_map(
        shards,
        mesh=mesh,
        in_specs=(
            P(("groups", "band"), "tiles", None, None, None),
            P(("groups", "band"), "tiles", None, None, None),
            P("tiles"),
            P("tiles", None),
            P("tiles", None),
            P(("groups", "tiles", "band"), None, None, None),
            P(),
            P(),
            P(),
            P(),
            P(),
            P(),
            P(),
            P(),
            P(),
        ),
        out_specs=(
            P(("groups", "band"), "tiles", "rep", None, None),
            P(("groups", "tiles", "band"), None, None, None),
        ),
        check_vma=False,
    )
```

```python
import jax
import jax.numpy as jnp
from jax import lax
from jax.sharding import PartitionSpec as P


def padded(block, sides, width):
    for axis, dim in sides:
        count = lax.axis_size(axis)
        forward = [(i, i + 1) for i in range(count - 1)]
        backward = [(target, source) for source, target in forward]
        low = lax.ppermute(
            lax.slice_in_dim(block, block.shape[dim] - width, None, axis=dim), axis, forward
        )
        high = lax.ppermute(lax.slice_in_dim(block, 0, width, axis=dim), axis, backward)
        block = jnp.concatenate([low, block, high], axis=dim)
    return block


def apply_filter(
    padded_input, filter_weight, dilation_rate, first_row_index, row_count, column_count
):
    total = None
    for left_operand in (-1, 0, 1):
        for right_operand in (-1, 0, 1):
            window_slice = padded_input[
                :,
                :,
                :,
                first_row_index
                + left_operand * dilation_rate : first_row_index
                + left_operand * dilation_rate
                + row_count,
                2
                + right_operand * dilation_rate : 2
                + right_operand * dilation_rate
                + column_count,
            ]
            term = jnp.einsum(
                "oi,bsirw->bsorw",
                filter_weight[(left_operand + 1) * 3 + (right_operand + 1)],
                window_slice,
                preferred_element_type=jnp.float32,
            )
            total = term if total is None else total + term
    return total


def conv(images, filter_weight, dilation_rate):
    taps, outs, ins = filter_weight.shape
    kernel = filter_weight.reshape(3, 3, outs, ins).transpose(2, 3, 0, 1)
    return lax.conv_general_dilated(
        images,
        kernel,
        window_strides=(1, 1),
        padding="VALID",
        rhs_dilation=(dilation_rate, dilation_rate),
        dimension_numbers=("NCHW", "OIHW", "NCHW"),
        preferred_element_type=jnp.float32,
    )


def choose_rows(block, select):
    masked = jnp.where(select[None, :, None, None, None], block, jnp.zeros_like(block))
    return jnp.sum(masked, axis=1)


def exchange_sum(part, owned):
    bands = lax.axis_size("band")
    reps = lax.axis_size("rep")
    band = lax.axis_index("band")
    total = None
    for shift in range(bands):
        pair = None
        for step in range(reps):
            target = (band + shift) % bands
            chunk = lax.dynamic_slice_in_dim(part, target * owned, owned, 0)
            if shift or step:
                perm = [
                    (b * reps + r, ((b + shift) % bands) * reps + (r + step) % reps)
                    for b in range(bands)
                    for r in range(reps)
                ]
                chunk = lax.ppermute(chunk, ("band", "rep"), perm)
            pair = chunk if pair is None else pair + chunk
        total = pair if total is None else total + pair
    return total


def shards(
    features,
    state,
    live,
    neighbours,
    coarse_perm,
    coarse_state,
    w_update,
    b_update,
    w_reset,
    b_reset,
    w_cand,
    b_cand,
    u_pool,
    u_state,
    b_coarse,
):
    slots = state.shape[1]
    chans = state.shape[2]
    row_count = state.shape[3]
    column_count = state.shape[4]
    inputs_count = features.shape[2]
    half = chans // lax.axis_size("rep")
    start = lax.axis_index("rep") * half
    base = lax.axis_index("tiles") * slots
    ups = neighbours[:, 0]
    downs = neighbours[:, 1]
    up_here = (ups >= base) & (ups < base + slots)
    down_here = (downs >= base) & (downs < base + slots)
    up_far = (ups >= 0) & jnp.logical_not(up_here)
    down_far = (downs >= 0) & jnp.logical_not(down_here)
    alive = live > 0
    first_sel = alive & jnp.logical_not(up_here)
    last_sel = alive & jnp.logical_not(down_here)

    def own_out(filter_weight):
        return lax.dynamic_slice_in_dim(filter_weight, start, half, 1)

    def own_bias(bias):
        return lax.dynamic_slice_in_dim(bias, start, half, 0)[:, None, None]

    hb = state.astype(jnp.bfloat16)
    joined = jnp.concatenate([features, hb], axis=2)
    top = choose_rows(joined[:, :, :, :3, :], first_sel)
    bottom = choose_rows(joined[:, :, :, row_count - 3 :, :], last_sel)
    cycle = padded(jnp.concatenate([top, bottom], axis=2), (("tiles", 2),), 3)
    cycle_prev = cycle[:, None, :, :3, :]
    cycle_next = cycle[:, None, :, 3 * 3 : 4 * 3, :]
    top_local = jnp.take(
        joined[:, :, :, row_count - 3 :, :], jnp.clip(ups - base, 0, slots - 1), axis=1
    )
    bottom_local = jnp.take(joined[:, :, :, :3, :], jnp.clip(downs - base, 0, slots - 1), axis=1)
    zeros_rows = jnp.zeros_like(top_local)
    top = jnp.where(
        up_here[None, :, None, None, None],
        top_local,
        jnp.where(up_far[None, :, None, None, None], cycle_prev + zeros_rows, zeros_rows),
    )
    bottom = jnp.where(
        down_here[None, :, None, None, None],
        bottom_local,
        jnp.where(down_far[None, :, None, None, None], cycle_next + zeros_rows, zeros_rows),
    )
    full = jnp.concatenate([top, joined, bottom], axis=3)
    first = jnp.pad(full, ((0, 0), (0, 0), (0, 0), (0, 0), (2, 2)))
    band_local = first.shape[0]
    images = band_local * slots
    flat = first.reshape((images,) + first.shape[2:])
    gates = conv(
        flat[:, :, :, 1 : column_count + 3],
        jnp.concatenate([own_out(w_update), w_reset], axis=1),
        1,
    )
    gate_bias = jnp.concatenate([own_bias(b_update), b_reset[:, None, None]], axis=0)
    gates = jax.nn.sigmoid(gates + gate_bias)
    update = gates[:, :half, 2 : row_count + 2].reshape((band_local, slots, half, row_count, column_count))
    reset = gates[:, half:]
    hidden_wide = flat[:, inputs_count:, 1 : row_count + 5, 2 : column_count + 2]
    gated = (reset * hidden_wide.astype(jnp.float32)).astype(jnp.bfloat16)
    gated_pad = jnp.pad(gated, ((0, 0), (0, 0), (0, 0), (2, 2)))
    second = jnp.concatenate([flat[:, :inputs_count, 1 : row_count + 5, :], gated_pad], axis=1)
    candidate = jnp.tanh(conv(second, own_out(w_cand), 2) + own_bias(b_cand))
    candidate = candidate.reshape((band_local, slots, half, row_count, column_count))
    state_half = lax.dynamic_slice_in_dim(state, start, half, 2)
    live_scale = alive.astype(jnp.float32)[None, :, None, None, None]
    new_half = ((1.0 - update) * state_half + update * candidate) * live_scale
    summed = jnp.sum(new_half, axis=0)
    column_pool = (
        jnp.arange(column_count)[:, None] // 4 == jnp.arange(column_count // 4)[None, :]
    ).astype(jnp.float32)
    cols = jnp.einsum(
        "schw,wj->schj", summed, column_pool, precision=lax.Precision.HIGHEST
    )
    pooled = jnp.sum(
        cols.reshape(slots, half, row_count // 4, 4, column_count // 4), axis=3
    ) / 16.0
    ordered = jnp.take(pooled, coarse_perm[0], axis=0)
    part = jnp.einsum(
        "oc,kcij->koij",
        lax.dynamic_slice_in_dim(u_pool, start, half, 1),
        ordered,
        precision=lax.Precision.HIGHEST,
    )
    pre = exchange_sum(part, coarse_state.shape[0])
    pre = pre + jnp.einsum("oc,kcij->koij", u_state, coarse_state, precision=lax.Precision.HIGHEST)
    pre = pre + b_coarse[None, :, None, None]
    coarse_next = coarse_state + jnp.tanh(pre)
    return (new_half, coarse_next)


def solution(mesh):
    return jax.shard_map(
        shards,
        mesh=mesh,
        in_specs=(
            P(("groups", "band"), "tiles", None, None, None),
            P(("groups", "band"), "tiles", None, None, None),
            P("tiles"),
            P("tiles", None),
            P("tiles", None),
            P(("groups", "tiles", "band"), None, None, None),
            P(),
            P(),
            P(),
            P(),
            P(),
            P(),
            P(),
            P(),
            P(),
        ),
        out_specs=(
            P(("groups", "band"), "tiles", "rep", None, None),
            P(("groups", "tiles", "band"), None, None, None),
        ),
        check_vma=False,
    )
```

```python
import jax
import jax.numpy as jnp
from jax import lax
from jax.sharding import PartitionSpec as P


def padded(block, sides, width):
    for axis, dim in sides:
        count = lax.axis_size(axis)
        forward = [(i, i + 1) for i in range(count - 1)]
        backward = [(target, source) for source, target in forward]
        low = lax.ppermute(
            lax.slice_in_dim(block, block.shape[dim] - width, None, axis=dim), axis, forward
        )
        high = lax.ppermute(lax.slice_in_dim(block, 0, width, axis=dim), axis, backward)
        block = jnp.concatenate([low, block, high], axis=dim)
    return block


def apply_filter(
    padded_input, filter_weight, dilation_rate, first_row_index, row_count, column_count
):
    total = None
    for left_operand in (-1, 0, 1):
        for right_operand in (-1, 0, 1):
            window_slice = padded_input[
                :,
                :,
                :,
                first_row_index
                + left_operand * dilation_rate : first_row_index
                + left_operand * dilation_rate
                + row_count,
                2
                + right_operand * dilation_rate : 2
                + right_operand * dilation_rate
                + column_count,
            ]
            term = jnp.einsum(
                "oi,bsirw->bsorw",
                filter_weight[(left_operand + 1) * 3 + (right_operand + 1)],
                window_slice,
                preferred_element_type=jnp.float32,
            )
            total = term if total is None else total + term
    return total


def choose_rows(block, select):
    masked = jnp.where(select[None, :, None, None, None], block, jnp.zeros_like(block))
    return jnp.sum(masked, axis=1)


def exchange_sum(part, owned):
    bands = lax.axis_size("band")
    reps = lax.axis_size("rep")
    band = lax.axis_index("band")
    total = None
    for shift in range(bands):
        pair = None
        for step in range(reps):
            target = (band + shift) % bands
            chunk = lax.dynamic_slice_in_dim(part, target * owned, owned, 0)
            if shift or step:
                perm = [
                    (b * reps + r, ((b + shift) % bands) * reps + (r + step) % reps)
                    for b in range(bands)
                    for r in range(reps)
                ]
                chunk = lax.ppermute(chunk, ("band", "rep"), perm)
            pair = chunk if pair is None else pair + chunk
        total = pair if total is None else total + pair
    return total


def shards(
    features,
    state,
    live,
    neighbours,
    coarse_perm,
    coarse_state,
    w_update,
    b_update,
    w_reset,
    b_reset,
    w_cand,
    b_cand,
    u_pool,
    u_state,
    b_coarse,
):
    slots = state.shape[1]
    chans = state.shape[2]
    row_count = state.shape[3]
    column_count = state.shape[4]
    inputs_count = features.shape[2]
    half = chans // lax.axis_size("rep")
    start = lax.axis_index("rep") * half
    base = lax.axis_index("tiles") * slots
    ups = neighbours[:, 0]
    downs = neighbours[:, 1]
    up_here = (ups >= base) & (ups < base + slots)
    down_here = (downs >= base) & (downs < base + slots)
    up_far = (ups >= 0) & jnp.logical_not(up_here)
    down_far = (downs >= 0) & jnp.logical_not(down_here)
    alive = live > 0
    first_sel = alive & jnp.logical_not(up_here)
    last_sel = alive & jnp.logical_not(down_here)

    def own_out(filter_weight):
        return lax.dynamic_slice_in_dim(filter_weight, start, half, 1)

    def own_bias(bias):
        return lax.dynamic_slice_in_dim(bias, start, half, 0)[:, None, None]

    hb = state.astype(jnp.bfloat16)
    joined = jnp.concatenate([features, hb], axis=2)
    top = choose_rows(joined[:, :, :, :3, :], first_sel)
    bottom = choose_rows(joined[:, :, :, row_count - 3 :, :], last_sel)
    cycle = padded(jnp.concatenate([top, bottom], axis=2), (("tiles", 2),), 3)
    cycle_prev = cycle[:, None, :, :3, :]
    cycle_next = cycle[:, None, :, 3 * 3 : 4 * 3, :]
    top_local = jnp.take(
        joined[:, :, :, row_count - 3 :, :], jnp.clip(ups - base, 0, slots - 1), axis=1
    )
    bottom_local = jnp.take(joined[:, :, :, :3, :], jnp.clip(downs - base, 0, slots - 1), axis=1)
    zeros_rows = jnp.zeros_like(top_local)
    top = jnp.where(
        up_here[None, :, None, None, None],
        top_local,
        jnp.where(up_far[None, :, None, None, None], cycle_prev + zeros_rows, zeros_rows),
    )
    bottom = jnp.where(
        down_here[None, :, None, None, None],
        bottom_local,
        jnp.where(down_far[None, :, None, None, None], cycle_next + zeros_rows, zeros_rows),
    )
    full = jnp.concatenate([top, joined, bottom], axis=3)
    first = jnp.pad(full, ((0, 0), (0, 0), (0, 0), (0, 0), (2, 2)))
    update = jax.nn.sigmoid(
        apply_filter(first, own_out(w_update), 1, 3, row_count, column_count) + own_bias(b_update)
    )
    hidden_wide = first[:, :, inputs_count:, 1 : row_count + 5, 2 : column_count + 2]
    reset = jax.nn.sigmoid(
        apply_filter(first, w_reset, 1, 1, row_count + 4, column_count) + b_reset[:, None, None]
    )
    gated = (reset * hidden_wide.astype(jnp.float32)).astype(jnp.bfloat16)
    gated_pad = jnp.pad(gated, ((0, 0), (0, 0), (0, 0), (0, 0), (2, 2)))
    second = jnp.concatenate([first[:, :, :inputs_count, 1 : row_count + 5, :], gated_pad], axis=2)
    candidate = jnp.tanh(
        apply_filter(second, own_out(w_cand), 2, 2, row_count, column_count) + own_bias(b_cand)
    )
    state_half = lax.dynamic_slice_in_dim(state, start, half, 2)
    live_scale = alive.astype(jnp.float32)[None, :, None, None, None]
    new_half = ((1.0 - update) * state_half + update * candidate) * live_scale
    summed = jnp.sum(new_half, axis=0)
    column_pool = (
        jnp.arange(column_count)[:, None] // 4 == jnp.arange(column_count // 4)[None, :]
    ).astype(jnp.float32)
    cols = jnp.einsum(
        "schw,wj->schj", summed, column_pool, precision=lax.Precision.HIGHEST
    )
    pooled = jnp.sum(
        cols.reshape(slots, half, row_count // 4, 4, column_count // 4), axis=3
    ) / 16.0
    ordered = jnp.take(pooled, coarse_perm[0], axis=0)
    part = jnp.einsum(
        "oc,kcij->koij",
        lax.dynamic_slice_in_dim(u_pool, start, half, 1),
        ordered,
        precision=lax.Precision.HIGHEST,
    )
    pre = exchange_sum(part, coarse_state.shape[0])
    pre = pre + jnp.einsum("oc,kcij->koij", u_state, coarse_state, precision=lax.Precision.HIGHEST)
    pre = pre + b_coarse[None, :, None, None]
    coarse_next = coarse_state + jnp.tanh(pre)
    return (new_half, coarse_next)


def solution(mesh):
    return jax.shard_map(
        shards,
        mesh=mesh,
        in_specs=(
            P(("groups", "band"), "tiles", None, None, None),
            P(("groups", "band"), "tiles", None, None, None),
            P("tiles"),
            P("tiles", None),
            P("tiles", None),
            P(("groups", "tiles", "band"), None, None, None),
            P(),
            P(),
            P(),
            P(),
            P(),
            P(),
            P(),
            P(),
            P(),
        ),
        out_specs=(
            P(("groups", "band"), "tiles", "rep", None, None),
            P(("groups", "tiles", "band"), None, None, None),
        ),
        check_vma=False,
    )
```

```python
import jax
import jax.numpy as jnp
from jax import lax
from jax.sharding import PartitionSpec as P


def padded(block, sides, width):
    for axis, dim in sides:
        count = lax.axis_size(axis)
        forward = [(i, i + 1) for i in range(count - 1)]
        backward = [(target, source) for source, target in forward]
        low = lax.ppermute(
            lax.slice_in_dim(block, block.shape[dim] - width, None, axis=dim), axis, forward
        )
        high = lax.ppermute(lax.slice_in_dim(block, 0, width, axis=dim), axis, backward)
        block = jnp.concatenate([low, block, high], axis=dim)
    return block


def apply_filter(
    padded_input, filter_weight, dilation_rate, first_row_index, row_count, column_count
):
    total = None
    for left_operand in (-1, 0, 1):
        for right_operand in (-1, 0, 1):
            window_slice = padded_input[
                :,
                :,
                :,
                first_row_index
                + left_operand * dilation_rate : first_row_index
                + left_operand * dilation_rate
                + row_count,
                2
                + right_operand * dilation_rate : 2
                + right_operand * dilation_rate
                + column_count,
            ]
            term = jnp.einsum(
                "oi,bsirw->bsorw",
                filter_weight[(left_operand + 1) * 3 + (right_operand + 1)],
                window_slice,
                preferred_element_type=jnp.float32,
            )
            total = term if total is None else total + term
    return total


def choose_rows(block, select):
    masked = jnp.where(select[None, :, None, None, None], block, jnp.zeros_like(block))
    return jnp.sum(masked, axis=1)


def exchange_sum(part, owned):
    bands = lax.axis_size("band")
    band = lax.axis_index("band")
    total = None
    for shift in range(bands):
        target = (band + shift) % bands
        chunk = lax.dynamic_slice_in_dim(part, target * owned, owned, 0)
        if shift:
            perm = [(b, (b + shift) % bands) for b in range(bands)]
            chunk = lax.ppermute(chunk, "band", perm)
        total = chunk if total is None else total + chunk
    return total


def shards(
    features,
    state,
    live,
    neighbours,
    coarse_perm,
    coarse_state,
    w_update,
    b_update,
    w_reset,
    b_reset,
    w_cand,
    b_cand,
    u_pool,
    u_state,
    b_coarse,
):
    slots = state.shape[1]
    chans = state.shape[2]
    row_count = state.shape[3]
    column_count = state.shape[4]
    inputs_count = features.shape[2]
    half = chans // lax.axis_size("rep")
    start = lax.axis_index("rep") * half
    base = lax.axis_index("tiles") * slots
    ups = neighbours[:, 0]
    downs = neighbours[:, 1]
    up_here = (ups >= base) & (ups < base + slots)
    down_here = (downs >= base) & (downs < base + slots)
    up_far = (ups >= 0) & jnp.logical_not(up_here)
    down_far = (downs >= 0) & jnp.logical_not(down_here)
    alive = live > 0
    first_sel = alive & jnp.logical_not(up_here)
    last_sel = alive & jnp.logical_not(down_here)

    def own_out(filter_weight):
        return lax.dynamic_slice_in_dim(filter_weight, start, half, 1)

    def own_bias(bias):
        return lax.dynamic_slice_in_dim(bias, start, half, 0)[:, None, None]

    hb = state.astype(jnp.bfloat16)
    joined = jnp.concatenate([features, hb], axis=2)
    top = choose_rows(joined[:, :, :, :3, :], first_sel)
    bottom = choose_rows(joined[:, :, :, row_count - 3 :, :], last_sel)
    cycle = padded(jnp.concatenate([top, bottom], axis=2), (("tiles", 2),), 3)
    cycle_prev = cycle[:, None, :, :3, :]
    cycle_next = cycle[:, None, :, 3 * 3 : 4 * 3, :]
    top_local = jnp.take(
        joined[:, :, :, row_count - 3 :, :], jnp.clip(ups - base, 0, slots - 1), axis=1
    )
    bottom_local = jnp.take(joined[:, :, :, :3, :], jnp.clip(downs - base, 0, slots - 1), axis=1)
    zeros_rows = jnp.zeros_like(top_local)
    top = jnp.where(
        up_here[None, :, None, None, None],
        top_local,
        jnp.where(up_far[None, :, None, None, None], cycle_prev + zeros_rows, zeros_rows),
    )
    bottom = jnp.where(
        down_here[None, :, None, None, None],
        bottom_local,
        jnp.where(down_far[None, :, None, None, None], cycle_next + zeros_rows, zeros_rows),
    )
    full = jnp.concatenate([top, joined, bottom], axis=3)
    first = jnp.pad(full, ((0, 0), (0, 0), (0, 0), (0, 0), (2, 2)))
    update = jax.nn.sigmoid(
        apply_filter(first, w_update, 1, 3, row_count, column_count) + b_update[:, None, None]
    )
    hidden_wide = first[:, :, inputs_count:, 1 : row_count + 5, 2 : column_count + 2]
    reset = jax.nn.sigmoid(
        apply_filter(first, w_reset, 1, 1, row_count + 4, column_count) + b_reset[:, None, None]
    )
    gated = (reset * hidden_wide.astype(jnp.float32)).astype(jnp.bfloat16)
    gated_pad = jnp.pad(gated, ((0, 0), (0, 0), (0, 0), (0, 0), (2, 2)))
    second = jnp.concatenate([first[:, :, :inputs_count, 1 : row_count + 5, :], gated_pad], axis=2)
    candidate = jnp.tanh(
        apply_filter(second, w_cand, 2, 2, row_count, column_count) + b_cand[:, None, None]
    )
    live_scale = alive.astype(jnp.float32)[None, :, None, None, None]
    new_state = ((1.0 - update) * state + update * candidate) * live_scale
    new_half = lax.dynamic_slice_in_dim(new_state, start, half, 2)
    summed = jnp.sum(new_state, axis=0)
    column_pool = (
        jnp.arange(column_count)[:, None] // 4 == jnp.arange(column_count // 4)[None, :]
    ).astype(jnp.float32)
    cols = jnp.einsum(
        "schw,wj->schj", summed, column_pool, precision=lax.Precision.HIGHEST
    )
    pooled = jnp.sum(
        cols.reshape(slots, chans, row_count // 4, 4, column_count // 4), axis=3
    ) / 16.0
    ordered = jnp.take(pooled, coarse_perm[0], axis=0)
    part = jnp.einsum("oc,kcij->koij", u_pool, ordered, precision=lax.Precision.HIGHEST)
    pre = exchange_sum(part, coarse_state.shape[0])
    pre = pre + jnp.einsum("oc,kcij->koij", u_state, coarse_state, precision=lax.Precision.HIGHEST)
    pre = pre + b_coarse[None, :, None, None]
    coarse_next = coarse_state + jnp.tanh(pre)
    return (new_half, coarse_next)


def solution(mesh):
    return jax.shard_map(
        shards,
        mesh=mesh,
        in_specs=(
            P(("groups", "band"), "tiles", None, None, None),
            P(("groups", "band"), "tiles", None, None, None),
            P("tiles"),
            P("tiles", None),
            P("tiles", None),
            P(("groups", "tiles", "band"), None, None, None),
            P(),
            P(),
            P(),
            P(),
            P(),
            P(),
            P(),
            P(),
            P(),
        ),
        out_specs=(
            P(("groups", "band"), "tiles", "rep", None, None),
            P(("groups", "tiles", "band"), None, None, None),
        ),
        check_vma=False,
    )
```

```python
import jax
import jax.numpy as jnp
from jax import lax
from jax.sharding import PartitionSpec as P


def padded(block, sides, width):
    for axis, dim in sides:
        count = lax.axis_size(axis)
        forward = [(i, i + 1) for i in range(count - 1)]
        backward = [(target, source) for source, target in forward]
        low = lax.ppermute(
            lax.slice_in_dim(block, block.shape[dim] - width, None, axis=dim), axis, forward
        )
        high = lax.ppermute(lax.slice_in_dim(block, 0, width, axis=dim), axis, backward)
        block = jnp.concatenate([low, block, high], axis=dim)
    return block


def apply_filter(
    padded_input, filter_weight, dilation_rate, first_row_index, row_count, column_count
):
    offsets = (-1, 0, 1)
    stacked = jnp.concatenate(
        [
            padded_input[
                :,
                :,
                :,
                first_row_index
                + row_offset * dilation_rate : first_row_index
                + row_offset * dilation_rate
                + row_count,
                :,
            ]
            for row_offset in offsets
        ],
        axis=2,
    )
    total = None
    for column_offset in offsets:
        weight = jnp.concatenate(
            [filter_weight[(row_offset + 1) * 3 + (column_offset + 1)] for row_offset in offsets],
            axis=1,
        )
        window_slice = stacked[
            ...,
            2 + column_offset * dilation_rate : 2 + column_offset * dilation_rate + column_count,
        ]
        term = jnp.einsum(
            "oi,bsirw->bsorw", weight, window_slice, preferred_element_type=jnp.float32
        )
        total = term if total is None else total + term
    return total


def choose_rows(block, select):
    masked = jnp.where(select[None, :, None, None, None], block, jnp.zeros_like(block))
    return jnp.sum(masked, axis=1)


def exchange_sum(part, owned):
    bands = lax.axis_size("band")
    band = lax.axis_index("band")
    total = None
    for shift in range(bands):
        target = (band + shift) % bands
        chunk = lax.dynamic_slice_in_dim(part, target * owned, owned, 0)
        if shift:
            perm = [(b, (b + shift) % bands) for b in range(bands)]
            chunk = lax.ppermute(chunk, "band", perm)
        total = chunk if total is None else total + chunk
    return total


def shards(
    features,
    state,
    live,
    neighbours,
    coarse_perm,
    coarse_state,
    w_update,
    b_update,
    w_reset,
    b_reset,
    w_cand,
    b_cand,
    u_pool,
    u_state,
    b_coarse,
):
    slots = state.shape[1]
    chans = state.shape[2]
    row_count = state.shape[3]
    column_count = state.shape[4]
    inputs_count = features.shape[2]
    half = chans // lax.axis_size("rep")
    start = lax.axis_index("rep") * half
    base = lax.axis_index("tiles") * slots
    ups = neighbours[:, 0]
    downs = neighbours[:, 1]
    up_here = (ups >= base) & (ups < base + slots)
    down_here = (downs >= base) & (downs < base + slots)
    up_far = (ups >= 0) & jnp.logical_not(up_here)
    down_far = (downs >= 0) & jnp.logical_not(down_here)
    alive = live > 0
    first_sel = alive & jnp.logical_not(up_here)
    last_sel = alive & jnp.logical_not(down_here)

    def own_out(filter_weight):
        return lax.dynamic_slice_in_dim(filter_weight, start, half, 1)

    def own_bias(bias):
        return lax.dynamic_slice_in_dim(bias, start, half, 0)[:, None, None]

    hb = state.astype(jnp.bfloat16)
    joined = jnp.concatenate([features, hb], axis=2)
    top = choose_rows(joined[:, :, :, :3, :], first_sel)
    bottom = choose_rows(joined[:, :, :, row_count - 3 :, :], last_sel)
    cycle = padded(jnp.concatenate([top, bottom], axis=2), (("tiles", 2),), 3)
    cycle_prev = cycle[:, None, :, :3, :]
    cycle_next = cycle[:, None, :, 3 * 3 : 4 * 3, :]
    top_local = jnp.take(
        joined[:, :, :, row_count - 3 :, :], jnp.clip(ups - base, 0, slots - 1), axis=1
    )
    bottom_local = jnp.take(joined[:, :, :, :3, :], jnp.clip(downs - base, 0, slots - 1), axis=1)
    zeros_rows = jnp.zeros_like(top_local)
    top = jnp.where(
        up_here[None, :, None, None, None],
        top_local,
        jnp.where(up_far[None, :, None, None, None], cycle_prev + zeros_rows, zeros_rows),
    )
    bottom = jnp.where(
        down_here[None, :, None, None, None],
        bottom_local,
        jnp.where(down_far[None, :, None, None, None], cycle_next + zeros_rows, zeros_rows),
    )
    full = jnp.concatenate([top, joined, bottom], axis=3)
    first = jnp.pad(full, ((0, 0), (0, 0), (0, 0), (0, 0), (2, 2)))
    gates = jax.nn.sigmoid(
        apply_filter(
            first,
            jnp.concatenate([w_update, w_reset], axis=1),
            1,
            1,
            row_count + 4,
            column_count,
        )
        + jnp.concatenate([b_update, b_reset])[:, None, None]
    )
    update = gates[:, :, :chans, 2 : row_count + 2]
    reset = gates[:, :, chans:]
    hidden_wide = first[:, :, inputs_count:, 1 : row_count + 5, 2 : column_count + 2]
    gated = (reset * hidden_wide.astype(jnp.float32)).astype(jnp.bfloat16)
    gated_pad = jnp.pad(gated, ((0, 0), (0, 0), (0, 0), (0, 0), (2, 2)))
    second = jnp.concatenate([first[:, :, :inputs_count, 1 : row_count + 5, :], gated_pad], axis=2)
    candidate = jnp.tanh(
        apply_filter(second, w_cand, 2, 2, row_count, column_count) + b_cand[:, None, None]
    )
    live_scale = alive.astype(jnp.float32)[None, :, None, None, None]
    new_state = ((1.0 - update) * state + update * candidate) * live_scale
    new_half = lax.dynamic_slice_in_dim(new_state, start, half, 2)
    summed = jnp.sum(new_state, axis=0)
    column_pool = (
        jnp.arange(column_count)[:, None] // 4 == jnp.arange(column_count // 4)[None, :]
    ).astype(jnp.float32)
    cols = jnp.einsum(
        "schw,wj->schj", summed, column_pool, precision=lax.Precision.HIGHEST
    )
    pooled = jnp.sum(
        cols.reshape(slots, chans, row_count // 4, 4, column_count // 4), axis=3
    ) / 16.0
    ordered = jnp.take(pooled, coarse_perm[0], axis=0)
    part = jnp.einsum("oc,kcij->koij", u_pool, ordered, precision=lax.Precision.HIGHEST)
    pre = exchange_sum(part, coarse_state.shape[0])
    pre = pre + jnp.einsum("oc,kcij->koij", u_state, coarse_state, precision=lax.Precision.HIGHEST)
    pre = pre + b_coarse[None, :, None, None]
    coarse_next = coarse_state + jnp.tanh(pre)
    return (new_half, coarse_next)


def solution(mesh):
    return jax.shard_map(
        shards,
        mesh=mesh,
        in_specs=(
            P(("groups", "band"), "tiles", None, None, None),
            P(("groups", "band"), "tiles", None, None, None),
            P("tiles"),
            P("tiles", None),
            P("tiles", None),
            P(("groups", "tiles", "band"), None, None, None),
            P(),
            P(),
            P(),
            P(),
            P(),
            P(),
            P(),
            P(),
            P(),
        ),
        out_specs=(
            P(("groups", "band"), "tiles", "rep", None, None),
            P(("groups", "tiles", "band"), None, None, None),
        ),
        check_vma=False,
    )
```

```python
import jax
import jax.numpy as jnp
from jax import lax
from jax.sharding import PartitionSpec as P
from jax.experimental import pallas as pl


def padded(block, sides, width):
    for axis, dim in sides:
        count = lax.axis_size(axis)
        forward = [(i, i + 1) for i in range(count - 1)]
        backward = [(target, source) for source, target in forward]
        low = lax.ppermute(
            lax.slice_in_dim(block, block.shape[dim] - width, None, axis=dim), axis, forward
        )
        high = lax.ppermute(lax.slice_in_dim(block, 0, width, axis=dim), axis, backward)
        block = jnp.concatenate([low, block, high], axis=dim)
    return block


def apply_filter(
    padded_input, filter_weight, dilation_rate, first_row_index, row_count, column_count
):
    total = None
    for left_operand in (-1, 0, 1):
        for right_operand in (-1, 0, 1):
            window_slice = padded_input[
                :,
                :,
                :,
                first_row_index
                + left_operand * dilation_rate : first_row_index
                + left_operand * dilation_rate
                + row_count,
                2
                + right_operand * dilation_rate : 2
                + right_operand * dilation_rate
                + column_count,
            ]
            term = jnp.einsum(
                "oi,bsirw->bsorw",
                filter_weight[(left_operand + 1) * 3 + (right_operand + 1)],
                window_slice,
                preferred_element_type=jnp.float32,
            )
            total = term if total is None else total + term
    return total


PADW = 132
WIDE = 2688
OUT = 2176
MARGIN = 128


def gru_kernel(x_ref, wg_ref, bg_ref, wcf_ref, wcg_ref, bc_ref, upd_ref, cand_ref):
    width = PADW
    x = x_ref[0]
    acc = None
    for a in (-1, 0, 1):
        for b in (-1, 0, 1):
            off = (1 + a) * width + 2 + b
            term = jnp.dot(
                wg_ref[(a + 1) * 3 + (b + 1)], x[:, off : off + WIDE],
                preferred_element_type=jnp.float32,
            )
            acc = term if acc is None else acc + term
    gates = jax.nn.sigmoid(acc + bg_ref[...])
    chans = gates.shape[0] // 2
    hidden = x[:chans, width + 2 : width + 2 + WIDE].astype(jnp.float32)
    col = lax.broadcasted_iota(jnp.int32, (chans, WIDE), 1) % width
    gated = jnp.where(col < width - 4, gates[chans:] * hidden, 0.0).astype(jnp.bfloat16)
    edge = jnp.zeros((chans, MARGIN), jnp.bfloat16)
    gm = jnp.concatenate([edge, gated, edge], axis=1)
    cacc = None
    for a in (-1, 0, 1):
        for b in (-1, 0, 1):
            tap = (a + 1) * 3 + (b + 1)
            xo = (3 + 2 * a) * width + 2 + 2 * b
            go = MARGIN + (2 + 2 * a) * width + 2 * b
            term = jnp.dot(
                wcf_ref[tap], x[:, xo : xo + OUT], preferred_element_type=jnp.float32
            ) + jnp.dot(wcg_ref[tap], gm[:, go : go + OUT], preferred_element_type=jnp.float32)
            cacc = term if cacc is None else cacc + term
    cand_ref[0] = jnp.tanh(cacc + bc_ref[...])
    upd_ref[0] = gates[:chans, 2 * width : 2 * width + OUT]


def choose_rows(block, select):
    masked = jnp.where(select[None, :, None, None, None], block, jnp.zeros_like(block))
    return jnp.sum(masked, axis=1)


def exchange_sum(part, owned):
    bands = lax.axis_size("band")
    band = lax.axis_index("band")
    total = None
    for shift in range(bands):
        target = (band + shift) % bands
        chunk = lax.dynamic_slice_in_dim(part, target * owned, owned, 0)
        if shift:
            perm = [(b, (b + shift) % bands) for b in range(bands)]
            chunk = lax.ppermute(chunk, "band", perm)
        total = chunk if total is None else total + chunk
    return total


def shards(
    features,
    state,
    live,
    neighbours,
    coarse_perm,
    coarse_state,
    w_update,
    b_update,
    w_reset,
    b_reset,
    w_cand,
    b_cand,
    u_pool,
    u_state,
    b_coarse,
):
    slots = state.shape[1]
    chans = state.shape[2]
    row_count = state.shape[3]
    column_count = state.shape[4]
    inputs_count = features.shape[2]
    half = chans // lax.axis_size("rep")
    start = lax.axis_index("rep") * half
    base = lax.axis_index("tiles") * slots
    ups = neighbours[:, 0]
    downs = neighbours[:, 1]
    up_here = (ups >= base) & (ups < base + slots)
    down_here = (downs >= base) & (downs < base + slots)
    up_far = (ups >= 0) & jnp.logical_not(up_here)
    down_far = (downs >= 0) & jnp.logical_not(down_here)
    alive = live > 0
    first_sel = alive & jnp.logical_not(up_here)
    last_sel = alive & jnp.logical_not(down_here)

    def own_out(filter_weight):
        return lax.dynamic_slice_in_dim(filter_weight, start, half, 1)

    def own_bias(bias):
        return lax.dynamic_slice_in_dim(bias, start, half, 0)[:, None, None]

    hb = state.astype(jnp.bfloat16)
    joined = jnp.concatenate([features, hb], axis=2)
    top = choose_rows(joined[:, :, :, :3, :], first_sel)
    bottom = choose_rows(joined[:, :, :, row_count - 3 :, :], last_sel)
    cycle = padded(jnp.concatenate([top, bottom], axis=2), (("tiles", 2),), 3)
    cycle_prev = cycle[:, None, :, :3, :]
    cycle_next = cycle[:, None, :, 3 * 3 : 4 * 3, :]
    top_local = jnp.take(
        joined[:, :, :, row_count - 3 :, :], jnp.clip(ups - base, 0, slots - 1), axis=1
    )
    bottom_local = jnp.take(joined[:, :, :, :3, :], jnp.clip(downs - base, 0, slots - 1), axis=1)
    zeros_rows = jnp.zeros_like(top_local)
    top = jnp.where(
        up_here[None, :, None, None, None],
        top_local,
        jnp.where(up_far[None, :, None, None, None], cycle_prev + zeros_rows, zeros_rows),
    )
    bottom = jnp.where(
        down_here[None, :, None, None, None],
        bottom_local,
        jnp.where(down_far[None, :, None, None, None], cycle_next + zeros_rows, zeros_rows),
    )
    full = jnp.concatenate([top, joined, bottom], axis=3)
    first = jnp.pad(full, ((0, 0), (0, 0), (0, 0), (0, 0), (2, 2)))
    band_local = first.shape[0]
    images = band_local * slots
    width = column_count + 4
    rows_first = row_count + 6
    cpad = 2 * chans
    reordered = jnp.concatenate(
        [first[:, :, inputs_count:], first[:, :, :inputs_count]], axis=2
    ).reshape(images, chans + inputs_count, rows_first * width)
    length = 128 * ((rows_first * width + 2 * width + 128) // 128)
    xin = jnp.pad(
        reordered,
        ((0, 0), (0, cpad - chans - inputs_count), (0, length - rows_first * width)),
    )

    def in_order(weight):
        moved = jnp.concatenate([weight[:, :, inputs_count:], weight[:, :, :inputs_count]], axis=2)
        return jnp.pad(moved, ((0, 0), (0, 0), (0, cpad - chans - inputs_count)))

    wg = jnp.concatenate([in_order(w_update), in_order(w_reset)], axis=1)
    bg = jnp.concatenate([b_update, b_reset])[:, None]
    wcf = jnp.pad(
        w_cand[:, :, :inputs_count], ((0, 0), (0, 0), (chans, cpad - chans - inputs_count))
    )
    wcg = w_cand[:, :, inputs_count:]
    bc = b_cand[:, None]
    full_spec = lambda shape: pl.BlockSpec(shape, lambda n: (0,) * len(shape))
    upd, cand = pl.pallas_call(
        gru_kernel,
        grid=(images,),
        in_specs=[
            pl.BlockSpec((1, cpad, length), lambda n: (n, 0, 0)),
            full_spec(wg.shape),
            full_spec(bg.shape),
            full_spec(wcf.shape),
            full_spec(wcg.shape),
            full_spec(bc.shape),
        ],
        out_specs=[
            pl.BlockSpec((1, chans, OUT), lambda n: (n, 0, 0)),
            pl.BlockSpec((1, chans, OUT), lambda n: (n, 0, 0)),
        ],
        out_shape=[
            jax.ShapeDtypeStruct((images, chans, OUT), jnp.float32),
            jax.ShapeDtypeStruct((images, chans, OUT), jnp.float32),
        ],
    )(xin, wg, bg, wcf, wcg, bc)

    def unflat(v):
        v = v[:, :, : row_count * width].reshape(images, chans, row_count, width)
        return v[..., :column_count].reshape(band_local, slots, chans, row_count, column_count)

    update = unflat(upd)
    candidate = unflat(cand)
    live_scale = alive.astype(jnp.float32)[None, :, None, None, None]
    new_state = ((1.0 - update) * state + update * candidate) * live_scale
    new_half = lax.dynamic_slice_in_dim(new_state, start, half, 2)
    summed = jnp.sum(new_state, axis=0)
    column_pool = (
        jnp.arange(column_count)[:, None] // 4 == jnp.arange(column_count // 4)[None, :]
    ).astype(jnp.float32)
    cols = jnp.einsum(
        "schw,wj->schj", summed, column_pool, precision=lax.Precision.HIGHEST
    )
    pooled = jnp.sum(
        cols.reshape(slots, chans, row_count // 4, 4, column_count // 4), axis=3
    ) / 16.0
    ordered = jnp.take(pooled, coarse_perm[0], axis=0)
    part = jnp.einsum("oc,kcij->koij", u_pool, ordered, precision=lax.Precision.HIGHEST)
    pre = exchange_sum(part, coarse_state.shape[0])
    pre = pre + jnp.einsum("oc,kcij->koij", u_state, coarse_state, precision=lax.Precision.HIGHEST)
    pre = pre + b_coarse[None, :, None, None]
    coarse_next = coarse_state + jnp.tanh(pre)
    return (new_half, coarse_next)


def solution(mesh):
    return jax.shard_map(
        shards,
        mesh=mesh,
        in_specs=(
            P(("groups", "band"), "tiles", None, None, None),
            P(("groups", "band"), "tiles", None, None, None),
            P("tiles"),
            P("tiles", None),
            P("tiles", None),
            P(("groups", "tiles", "band"), None, None, None),
            P(),
            P(),
            P(),
            P(),
            P(),
            P(),
            P(),
            P(),
            P(),
        ),
        out_specs=(
            P(("groups", "band"), "tiles", "rep", None, None),
            P(("groups", "tiles", "band"), None, None, None),
        ),
        check_vma=False,
    )
```

```python
import jax
import jax.numpy as jnp
from jax import lax
from jax.sharding import PartitionSpec as P


def padded(block, sides, width):
    for axis, dim in sides:
        count = lax.axis_size(axis)
        forward = [(i, i + 1) for i in range(count - 1)]
        backward = [(target, source) for source, target in forward]
        low = lax.ppermute(
            lax.slice_in_dim(block, block.shape[dim] - width, None, axis=dim), axis, forward
        )
        high = lax.ppermute(lax.slice_in_dim(block, 0, width, axis=dim), axis, backward)
        block = jnp.concatenate([low, block, high], axis=dim)
    return block


def apply_filter(
    padded_input, filter_weight, dilation_rate, first_row_index, row_count, column_count
):
    total = None
    for left_operand in (-1, 0, 1):
        for right_operand in (-1, 0, 1):
            window_slice = padded_input[
                :,
                :,
                :,
                first_row_index
                + left_operand * dilation_rate : first_row_index
                + left_operand * dilation_rate
                + row_count,
                2
                + right_operand * dilation_rate : 2
                + right_operand * dilation_rate
                + column_count,
            ]
            term = jnp.einsum(
                "oi,bsirw->bsorw",
                filter_weight[(left_operand + 1) * 3 + (right_operand + 1)],
                window_slice,
                preferred_element_type=jnp.float32,
            )
            total = term if total is None else total + term
    return total


def choose_rows(block, select):
    masked = jnp.where(select[None, :, None, None, None], block, jnp.zeros_like(block))
    return jnp.sum(masked, axis=1)


def pick_rows(rows, index):
    slots = rows.shape[1]
    hits = index[:, None] == jnp.arange(slots)[None, :]
    chosen = jnp.where(hits[None, :, :, None, None, None], rows[:, None], jnp.zeros_like(rows[:, None]))
    return jnp.sum(chosen, axis=2)


def exchange_sum(part, owned):
    bands = lax.axis_size("band")
    band = lax.axis_index("band")
    total = None
    for shift in range(bands):
        target = (band + shift) % bands
        chunk = lax.dynamic_slice_in_dim(part, target * owned, owned, 0)
        if shift:
            perm = [(b, (b + shift) % bands) for b in range(bands)]
            chunk = lax.ppermute(chunk, "band", perm)
        total = chunk if total is None else total + chunk
    return total


def shards(
    features,
    state,
    live,
    neighbours,
    coarse_perm,
    coarse_state,
    w_update,
    b_update,
    w_reset,
    b_reset,
    w_cand,
    b_cand,
    u_pool,
    u_state,
    b_coarse,
):
    slots = state.shape[1]
    chans = state.shape[2]
    row_count = state.shape[3]
    column_count = state.shape[4]
    inputs_count = features.shape[2]
    half = chans // lax.axis_size("rep")
    start = lax.axis_index("rep") * half
    base = lax.axis_index("tiles") * slots
    ups = neighbours[:, 0]
    downs = neighbours[:, 1]
    up_here = (ups >= base) & (ups < base + slots)
    down_here = (downs >= base) & (downs < base + slots)
    up_far = (ups >= 0) & jnp.logical_not(up_here)
    down_far = (downs >= 0) & jnp.logical_not(down_here)
    alive = live > 0
    first_sel = alive & jnp.logical_not(up_here)
    last_sel = alive & jnp.logical_not(down_here)

    def own_out(filter_weight):
        return lax.dynamic_slice_in_dim(filter_weight, start, half, 1)

    def own_bias(bias):
        return lax.dynamic_slice_in_dim(bias, start, half, 0)[:, None, None]

    hb = state.astype(jnp.bfloat16)
    joined = jnp.concatenate([features, hb], axis=2)
    top = choose_rows(joined[:, :, :, :3, :], first_sel)
    bottom = choose_rows(joined[:, :, :, row_count - 3 :, :], last_sel)
    cycle = padded(jnp.concatenate([top, bottom], axis=2), (("tiles", 2),), 3)
    cycle_prev = cycle[:, None, :, :3, :]
    cycle_next = cycle[:, None, :, 3 * 3 : 4 * 3, :]
    top_local = pick_rows(joined[:, :, :, row_count - 3 :, :], ups - base)
    bottom_local = pick_rows(joined[:, :, :, :3, :], downs - base)
    zeros_rows = jnp.zeros_like(top_local)
    top = jnp.where(
        up_here[None, :, None, None, None],
        top_local,
        jnp.where(up_far[None, :, None, None, None], cycle_prev + zeros_rows, zeros_rows),
    )
    bottom = jnp.where(
        down_here[None, :, None, None, None],
        bottom_local,
        jnp.where(down_far[None, :, None, None, None], cycle_next + zeros_rows, zeros_rows),
    )
    full = jnp.concatenate([top, joined, bottom], axis=3)
    first = jnp.pad(full, ((0, 0), (0, 0), (0, 0), (0, 0), (2, 2)))
    update = jax.nn.sigmoid(
        apply_filter(first, w_update, 1, 3, row_count, column_count) + b_update[:, None, None]
    )
    hidden_wide = first[:, :, inputs_count:, 1 : row_count + 5, 2 : column_count + 2]
    reset = jax.nn.sigmoid(
        apply_filter(first, w_reset, 1, 1, row_count + 4, column_count) + b_reset[:, None, None]
    )
    gated = (reset * hidden_wide.astype(jnp.float32)).astype(jnp.bfloat16)
    gated_pad = jnp.pad(gated, ((0, 0), (0, 0), (0, 0), (0, 0), (2, 2)))
    second = jnp.concatenate([first[:, :, :inputs_count, 1 : row_count + 5, :], gated_pad], axis=2)
    candidate = jnp.tanh(
        apply_filter(second, w_cand, 2, 2, row_count, column_count) + b_cand[:, None, None]
    )
    live_scale = alive.astype(jnp.float32)[None, :, None, None, None]
    new_state = ((1.0 - update) * state + update * candidate) * live_scale
    new_half = lax.dynamic_slice_in_dim(new_state, start, half, 2)
    summed = jnp.sum(new_state, axis=0)
    column_pool = (
        jnp.arange(column_count)[:, None] // 4 == jnp.arange(column_count // 4)[None, :]
    ).astype(jnp.float32)
    cols = jnp.einsum(
        "schw,wj->schj", summed, column_pool, precision=lax.Precision.HIGHEST
    )
    pooled = jnp.sum(
        cols.reshape(slots, chans, row_count // 4, 4, column_count // 4), axis=3
    ) / 16.0
    ordered = jnp.take(pooled, coarse_perm[0], axis=0)
    part = jnp.einsum("oc,kcij->koij", u_pool, ordered, precision=lax.Precision.HIGHEST)
    pre = exchange_sum(part, coarse_state.shape[0])
    pre = pre + jnp.einsum("oc,kcij->koij", u_state, coarse_state, precision=lax.Precision.HIGHEST)
    pre = pre + b_coarse[None, :, None, None]
    coarse_next = coarse_state + jnp.tanh(pre)
    return (new_half, coarse_next)


def solution(mesh):
    return jax.shard_map(
        shards,
        mesh=mesh,
        in_specs=(
            P(("groups", "band"), "tiles", None, None, None),
            P(("groups", "band"), "tiles", None, None, None),
            P("tiles"),
            P("tiles", None),
            P("tiles", None),
            P(("groups", "tiles", "band"), None, None, None),
            P(),
            P(),
            P(),
            P(),
            P(),
            P(),
            P(),
            P(),
            P(),
        ),
        out_specs=(
            P(("groups", "band"), "tiles", "rep", None, None),
            P(("groups", "tiles", "band"), None, None, None),
        ),
        check_vma=False,
    )
```

```python
import jax
import jax.numpy as jnp
from jax import lax
from jax.sharding import PartitionSpec as P


def padded(block, sides, width):
    for axis, dim in sides:
        count = lax.axis_size(axis)
        forward = [(i, i + 1) for i in range(count - 1)]
        backward = [(target, source) for source, target in forward]
        low = lax.ppermute(
            lax.slice_in_dim(block, block.shape[dim] - width, None, axis=dim), axis, forward
        )
        high = lax.ppermute(lax.slice_in_dim(block, 0, width, axis=dim), axis, backward)
        block = jnp.concatenate([low, block, high], axis=dim)
    return block


def apply_filter(
    padded_input, filter_weight, dilation_rate, first_row_index, row_count, column_count
):
    total = None
    for left_operand in (-1, 0, 1):
        for right_operand in (-1, 0, 1):
            window_slice = padded_input[
                :,
                :,
                :,
                first_row_index
                + left_operand * dilation_rate : first_row_index
                + left_operand * dilation_rate
                + row_count,
                2
                + right_operand * dilation_rate : 2
                + right_operand * dilation_rate
                + column_count,
            ]
            term = jnp.einsum(
                "oi,bsirw->bsorw",
                filter_weight[(left_operand + 1) * 3 + (right_operand + 1)],
                window_slice,
                preferred_element_type=jnp.float32,
            )
            total = term if total is None else total + term
    return total


def choose_rows(block, select):
    masked = jnp.where(select[None, :, None, None, None], block, jnp.zeros_like(block))
    return jnp.sum(masked, axis=1)


def exchange_sum(part, owned):
    bands = lax.axis_size("band")
    band = lax.axis_index("band")
    total = None
    for shift in range(bands):
        target = (band + shift) % bands
        chunk = lax.dynamic_slice_in_dim(part, target * owned, owned, 0)
        if shift:
            perm = [(b, (b + shift) % bands) for b in range(bands)]
            chunk = lax.ppermute(chunk, "band", perm)
        total = chunk if total is None else total + chunk
    return total


def shards(
    features,
    state,
    live,
    neighbours,
    coarse_perm,
    coarse_state,
    w_update,
    b_update,
    w_reset,
    b_reset,
    w_cand,
    b_cand,
    u_pool,
    u_state,
    b_coarse,
):
    slots = state.shape[1]
    chans = state.shape[2]
    row_count = state.shape[3]
    column_count = state.shape[4]
    inputs_count = features.shape[2]
    half = chans // lax.axis_size("rep")
    start = lax.axis_index("rep") * half
    base = lax.axis_index("tiles") * slots
    ups = neighbours[:, 0]
    downs = neighbours[:, 1]
    up_here = (ups >= base) & (ups < base + slots)
    down_here = (downs >= base) & (downs < base + slots)
    up_far = (ups >= 0) & jnp.logical_not(up_here)
    down_far = (downs >= 0) & jnp.logical_not(down_here)
    alive = live > 0
    first_sel = alive & jnp.logical_not(up_here)
    last_sel = alive & jnp.logical_not(down_here)

    def own_out(filter_weight):
        return lax.dynamic_slice_in_dim(filter_weight, start, half, 1)

    def own_bias(bias):
        return lax.dynamic_slice_in_dim(bias, start, half, 0)[:, None, None]

    hb = state.astype(jnp.bfloat16)
    joined = jnp.concatenate([features, hb], axis=2)
    top = choose_rows(joined[:, :, :, :3, :], first_sel)
    bottom = choose_rows(joined[:, :, :, row_count - 3 :, :], last_sel)
    cycle = padded(jnp.concatenate([top, bottom], axis=2), (("tiles", 2),), 3)
    cycle_prev = cycle[:, None, :, :3, :]
    cycle_next = cycle[:, None, :, 3 * 3 : 4 * 3, :]
    top_local = jnp.take(
        joined[:, :, :, row_count - 3 :, :], jnp.clip(ups - base, 0, slots - 1), axis=1
    )
    bottom_local = jnp.take(joined[:, :, :, :3, :], jnp.clip(downs - base, 0, slots - 1), axis=1)
    zeros_rows = jnp.zeros_like(top_local)
    top = jnp.where(
        up_here[None, :, None, None, None],
        top_local,
        jnp.where(up_far[None, :, None, None, None], cycle_prev + zeros_rows, zeros_rows),
    )
    bottom = jnp.where(
        down_here[None, :, None, None, None],
        bottom_local,
        jnp.where(down_far[None, :, None, None, None], cycle_next + zeros_rows, zeros_rows),
    )
    full = jnp.concatenate([top, joined, bottom], axis=3)
    first = jnp.pad(full, ((0, 0), (0, 0), (0, 0), (0, 0), (2, 2)))
    gates = jax.nn.sigmoid(
        apply_filter(
            first,
            jnp.concatenate([w_update, w_reset], axis=1),
            1,
            1,
            row_count + 4,
            column_count,
        )
        + jnp.concatenate([b_update, b_reset])[:, None, None]
    )
    update = gates[:, :, :chans, 2 : row_count + 2]
    reset = gates[:, :, chans:]
    hidden_wide = first[:, :, inputs_count:, 1 : row_count + 5, 2 : column_count + 2]
    gated = (reset * hidden_wide.astype(jnp.float32)).astype(jnp.bfloat16)
    gated_pad = jnp.pad(gated, ((0, 0), (0, 0), (0, 0), (0, 0), (2, 2)))
    second = jnp.concatenate([first[:, :, :inputs_count, 1 : row_count + 5, :], gated_pad], axis=2)
    candidate = jnp.tanh(
        apply_filter(second, w_cand, 2, 2, row_count, column_count) + b_cand[:, None, None]
    )
    live_scale = alive.astype(jnp.float32)[None, :, None, None, None]
    new_state = ((1.0 - update) * state + update * candidate) * live_scale
    new_half = lax.dynamic_slice_in_dim(new_state, start, half, 2)
    summed = jnp.sum(new_state, axis=0)
    column_pool = (
        jnp.arange(column_count)[:, None] // 4 == jnp.arange(column_count // 4)[None, :]
    ).astype(jnp.float32)
    cols = jnp.einsum(
        "schw,wj->schj", summed, column_pool, precision=lax.Precision.HIGHEST
    )
    pooled = jnp.sum(
        cols.reshape(slots, chans, row_count // 4, 4, column_count // 4), axis=3
    ) / 16.0
    ordered = jnp.take(pooled, coarse_perm[0], axis=0)
    part = jnp.einsum("oc,kcij->koij", u_pool, ordered, precision=lax.Precision.HIGHEST)
    pre = exchange_sum(part, coarse_state.shape[0])
    pre = pre + jnp.einsum("oc,kcij->koij", u_state, coarse_state, precision=lax.Precision.HIGHEST)
    pre = pre + b_coarse[None, :, None, None]
    coarse_next = coarse_state + jnp.tanh(pre)
    return (new_half, coarse_next)


def solution(mesh):
    return jax.shard_map(
        shards,
        mesh=mesh,
        in_specs=(
            P(("groups", "band"), "tiles", None, None, None),
            P(("groups", "band"), "tiles", None, None, None),
            P("tiles"),
            P("tiles", None),
            P("tiles", None),
            P(("groups", "tiles", "band"), None, None, None),
            P(),
            P(),
            P(),
            P(),
            P(),
            P(),
            P(),
            P(),
            P(),
        ),
        out_specs=(
            P(("groups", "band"), "tiles", "rep", None, None),
            P(("groups", "tiles", "band"), None, None, None),
        ),
        check_vma=False,
    )
```

```python
import jax
import jax.numpy as jnp
from jax import lax
from jax.sharding import PartitionSpec as P


def padded(block, sides, width):
    for axis, dim in sides:
        count = lax.axis_size(axis)
        forward = [(i, i + 1) for i in range(count - 1)]
        backward = [(target, source) for source, target in forward]
        low = lax.ppermute(
            lax.slice_in_dim(block, block.shape[dim] - width, None, axis=dim), axis, forward
        )
        high = lax.ppermute(lax.slice_in_dim(block, 0, width, axis=dim), axis, backward)
        block = jnp.concatenate([low, block, high], axis=dim)
    return block


def apply_filter(
    padded_input, filter_weight, dilation_rate, first_row_index, row_count, column_count
):
    total = None
    for left_operand in (-1, 0, 1):
        for right_operand in (-1, 0, 1):
            window_slice = padded_input[
                :,
                :,
                :,
                first_row_index
                + left_operand * dilation_rate : first_row_index
                + left_operand * dilation_rate
                + row_count,
                2
                + right_operand * dilation_rate : 2
                + right_operand * dilation_rate
                + column_count,
            ]
            term = jnp.einsum(
                "oi,bsirw->bsorw",
                filter_weight[(left_operand + 1) * 3 + (right_operand + 1)],
                window_slice,
                preferred_element_type=jnp.float32,
            )
            total = term if total is None else total + term
    return total


def choose_rows(block, select):
    masked = jnp.where(select[None, :, None, None, None], block, jnp.zeros_like(block))
    return jnp.sum(masked, axis=1)


def logistic(value):
    return 0.5 + 0.5 * jnp.tanh(0.5 * value)


def exchange_sum(part, owned):
    bands = lax.axis_size("band")
    band = lax.axis_index("band")
    total = None
    for shift in range(bands):
        target = (band + shift) % bands
        chunk = lax.dynamic_slice_in_dim(part, target * owned, owned, 0)
        if shift:
            perm = [(b, (b + shift) % bands) for b in range(bands)]
            chunk = lax.ppermute(chunk, "band", perm)
        total = chunk if total is None else total + chunk
    return total


def shards(
    features,
    state,
    live,
    neighbours,
    coarse_perm,
    coarse_state,
    w_update,
    b_update,
    w_reset,
    b_reset,
    w_cand,
    b_cand,
    u_pool,
    u_state,
    b_coarse,
):
    slots = state.shape[1]
    chans = state.shape[2]
    row_count = state.shape[3]
    column_count = state.shape[4]
    inputs_count = features.shape[2]
    half = chans // lax.axis_size("rep")
    start = lax.axis_index("rep") * half
    base = lax.axis_index("tiles") * slots
    ups = neighbours[:, 0]
    downs = neighbours[:, 1]
    up_here = (ups >= base) & (ups < base + slots)
    down_here = (downs >= base) & (downs < base + slots)
    up_far = (ups >= 0) & jnp.logical_not(up_here)
    down_far = (downs >= 0) & jnp.logical_not(down_here)
    alive = live > 0
    first_sel = alive & jnp.logical_not(up_here)
    last_sel = alive & jnp.logical_not(down_here)

    def own_out(filter_weight):
        return lax.dynamic_slice_in_dim(filter_weight, start, half, 1)

    def own_bias(bias):
        return lax.dynamic_slice_in_dim(bias, start, half, 0)[:, None, None]

    hb = state.astype(jnp.bfloat16)
    joined = jnp.concatenate([features, hb], axis=2)
    top = choose_rows(joined[:, :, :, :3, :], first_sel)
    bottom = choose_rows(joined[:, :, :, row_count - 3 :, :], last_sel)
    cycle = padded(jnp.concatenate([top, bottom], axis=2), (("tiles", 2),), 3)
    cycle_prev = cycle[:, None, :, :3, :]
    cycle_next = cycle[:, None, :, 3 * 3 : 4 * 3, :]
    top_local = jnp.take(
        joined[:, :, :, row_count - 3 :, :], jnp.clip(ups - base, 0, slots - 1), axis=1
    )
    bottom_local = jnp.take(joined[:, :, :, :3, :], jnp.clip(downs - base, 0, slots - 1), axis=1)
    zeros_rows = jnp.zeros_like(top_local)
    top = jnp.where(
        up_here[None, :, None, None, None],
        top_local,
        jnp.where(up_far[None, :, None, None, None], cycle_prev + zeros_rows, zeros_rows),
    )
    bottom = jnp.where(
        down_here[None, :, None, None, None],
        bottom_local,
        jnp.where(down_far[None, :, None, None, None], cycle_next + zeros_rows, zeros_rows),
    )
    full = jnp.concatenate([top, joined, bottom], axis=3)
    first = jnp.pad(full, ((0, 0), (0, 0), (0, 0), (0, 0), (2, 2)))
    gates = logistic(
        apply_filter(
            first,
            jnp.concatenate([w_update, w_reset], axis=1),
            1,
            1,
            row_count + 4,
            column_count,
        )
        + jnp.concatenate([b_update, b_reset])[:, None, None]
    )
    update = gates[:, :, :chans, 2 : row_count + 2]
    reset = gates[:, :, chans:]
    hidden_wide = first[:, :, inputs_count:, 1 : row_count + 5, 2 : column_count + 2]
    gated = (reset * hidden_wide.astype(jnp.float32)).astype(jnp.bfloat16)
    gated_pad = jnp.pad(gated, ((0, 0), (0, 0), (0, 0), (0, 0), (2, 2)))
    second = jnp.concatenate([first[:, :, :inputs_count, 1 : row_count + 5, :], gated_pad], axis=2)
    candidate = jnp.tanh(
        apply_filter(second, w_cand, 2, 2, row_count, column_count) + b_cand[:, None, None]
    )
    live_scale = alive.astype(jnp.float32)[None, :, None, None, None]
    new_state = ((1.0 - update) * state + update * candidate) * live_scale
    new_half = lax.dynamic_slice_in_dim(new_state, start, half, 2)
    summed = jnp.sum(new_state, axis=0)
    column_pool = (
        jnp.arange(column_count)[:, None] // 4 == jnp.arange(column_count // 4)[None, :]
    ).astype(jnp.float32)
    cols = jnp.einsum(
        "schw,wj->schj", summed, column_pool, precision=lax.Precision.HIGHEST
    )
    pooled = jnp.sum(
        cols.reshape(slots, chans, row_count // 4, 4, column_count // 4), axis=3
    ) / 16.0
    ordered = jnp.take(pooled, coarse_perm[0], axis=0)
    part = jnp.einsum("oc,kcij->koij", u_pool, ordered, precision=lax.Precision.HIGHEST)
    pre = exchange_sum(part, coarse_state.shape[0])
    pre = pre + jnp.einsum("oc,kcij->koij", u_state, coarse_state, precision=lax.Precision.HIGHEST)
    pre = pre + b_coarse[None, :, None, None]
    coarse_next = coarse_state + jnp.tanh(pre)
    return (new_half, coarse_next)


def solution(mesh):
    return jax.shard_map(
        shards,
        mesh=mesh,
        in_specs=(
            P(("groups", "band"), "tiles", None, None, None),
            P(("groups", "band"), "tiles", None, None, None),
            P("tiles"),
            P("tiles", None),
            P("tiles", None),
            P(("groups", "tiles", "band"), None, None, None),
            P(),
            P(),
            P(),
            P(),
            P(),
            P(),
            P(),
            P(),
            P(),
        ),
        out_specs=(
            P(("groups", "band"), "tiles", "rep", None, None),
            P(("groups", "tiles", "band"), None, None, None),
        ),
        check_vma=False,
    )
```

```python
import jax
import jax.numpy as jnp
from jax import lax
from jax.sharding import PartitionSpec as P


def padded(block, sides, width):
    for axis, dim in sides:
        count = lax.axis_size(axis)
        forward = [(i, i + 1) for i in range(count - 1)]
        backward = [(target, source) for source, target in forward]
        low = lax.ppermute(
            lax.slice_in_dim(block, block.shape[dim] - width, None, axis=dim), axis, forward
        )
        high = lax.ppermute(lax.slice_in_dim(block, 0, width, axis=dim), axis, backward)
        block = jnp.concatenate([low, block, high], axis=dim)
    return block


def apply_filter(
    padded_input, filter_weight, dilation_rate, first_row_index, row_count, column_count
):
    total = None
    for left_operand in (-1, 0, 1):
        for right_operand in (-1, 0, 1):
            window_slice = padded_input[
                :,
                :,
                :,
                first_row_index
                + left_operand * dilation_rate : first_row_index
                + left_operand * dilation_rate
                + row_count,
                2
                + right_operand * dilation_rate : 2
                + right_operand * dilation_rate
                + column_count,
            ]
            term = jnp.einsum(
                "oi,bsirw->bsorw",
                filter_weight[(left_operand + 1) * 3 + (right_operand + 1)],
                window_slice,
                preferred_element_type=jnp.float32,
            )
            total = term if total is None else total + term
    return total


def choose_rows(block, select):
    masked = jnp.where(select[None, :, None, None, None], block, jnp.zeros_like(block))
    return jnp.sum(masked, axis=1)


def logistic(value):
    return 0.5 + 0.5 * jnp.tanh(0.5 * value)


def channel_map(matrix, blocks):
    return jnp.sum(matrix[None, :, :, None, None] * blocks[:, None], axis=2)


def exchange_sum(part, owned):
    bands = lax.axis_size("band")
    band = lax.axis_index("band")
    total = None
    for shift in range(bands):
        target = (band + shift) % bands
        chunk = lax.dynamic_slice_in_dim(part, target * owned, owned, 0)
        if shift:
            perm = [(b, (b + shift) % bands) for b in range(bands)]
            chunk = lax.ppermute(chunk, "band", perm)
        total = chunk if total is None else total + chunk
    return total


def shards(
    features,
    state,
    live,
    neighbours,
    coarse_perm,
    coarse_state,
    w_update,
    b_update,
    w_reset,
    b_reset,
    w_cand,
    b_cand,
    u_pool,
    u_state,
    b_coarse,
):
    slots = state.shape[1]
    chans = state.shape[2]
    row_count = state.shape[3]
    column_count = state.shape[4]
    inputs_count = features.shape[2]
    half = chans // lax.axis_size("rep")
    start = lax.axis_index("rep") * half
    base = lax.axis_index("tiles") * slots
    ups = neighbours[:, 0]
    downs = neighbours[:, 1]
    up_here = (ups >= base) & (ups < base + slots)
    down_here = (downs >= base) & (downs < base + slots)
    up_far = (ups >= 0) & jnp.logical_not(up_here)
    down_far = (downs >= 0) & jnp.logical_not(down_here)
    alive = live > 0
    first_sel = alive & jnp.logical_not(up_here)
    last_sel = alive & jnp.logical_not(down_here)

    def own_out(filter_weight):
        return lax.dynamic_slice_in_dim(filter_weight, start, half, 1)

    def own_bias(bias):
        return lax.dynamic_slice_in_dim(bias, start, half, 0)[:, None, None]

    hb = state.astype(jnp.bfloat16)
    joined = jnp.concatenate([features, hb], axis=2)
    top = choose_rows(joined[:, :, :, :3, :], first_sel)
    bottom = choose_rows(joined[:, :, :, row_count - 3 :, :], last_sel)
    cycle = padded(jnp.concatenate([top, bottom], axis=2), (("tiles", 2),), 3)
    cycle_prev = cycle[:, None, :, :3, :]
    cycle_next = cycle[:, None, :, 3 * 3 : 4 * 3, :]
    top_local = jnp.take(
        joined[:, :, :, row_count - 3 :, :], jnp.clip(ups - base, 0, slots - 1), axis=1
    )
    bottom_local = jnp.take(joined[:, :, :, :3, :], jnp.clip(downs - base, 0, slots - 1), axis=1)
    zeros_rows = jnp.zeros_like(top_local)
    top = jnp.where(
        up_here[None, :, None, None, None],
        top_local,
        jnp.where(up_far[None, :, None, None, None], cycle_prev + zeros_rows, zeros_rows),
    )
    bottom = jnp.where(
        down_here[None, :, None, None, None],
        bottom_local,
        jnp.where(down_far[None, :, None, None, None], cycle_next + zeros_rows, zeros_rows),
    )
    full = jnp.concatenate([top, joined, bottom], axis=3)
    first = jnp.pad(full, ((0, 0), (0, 0), (0, 0), (0, 0), (2, 2)))
    gates = logistic(
        apply_filter(
            first,
            jnp.concatenate([w_update, w_reset], axis=1),
            1,
            1,
            row_count + 4,
            column_count,
        )
        + jnp.concatenate([b_update, b_reset])[:, None, None]
    )
    update = gates[:, :, :chans, 2 : row_count + 2]
    reset = gates[:, :, chans:]
    hidden_wide = first[:, :, inputs_count:, 1 : row_count + 5, 2 : column_count + 2]
    gated = (reset * hidden_wide.astype(jnp.float32)).astype(jnp.bfloat16)
    gated_pad = jnp.pad(gated, ((0, 0), (0, 0), (0, 0), (0, 0), (2, 2)))
    second = jnp.concatenate([first[:, :, :inputs_count, 1 : row_count + 5, :], gated_pad], axis=2)
    candidate = jnp.tanh(
        apply_filter(second, w_cand, 2, 2, row_count, column_count) + b_cand[:, None, None]
    )
    live_scale = alive.astype(jnp.float32)[None, :, None, None, None]
    new_state = ((1.0 - update) * state + update * candidate) * live_scale
    new_half = lax.dynamic_slice_in_dim(new_state, start, half, 2)
    summed = jnp.sum(new_state, axis=0)
    column_pool = (
        jnp.arange(column_count)[:, None] // 4 == jnp.arange(column_count // 4)[None, :]
    ).astype(jnp.float32)
    cols = jnp.einsum(
        "schw,wj->schj", summed, column_pool, precision=lax.Precision.HIGHEST
    )
    pooled = jnp.sum(
        cols.reshape(slots, chans, row_count // 4, 4, column_count // 4), axis=3
    ) / 16.0
    hits = coarse_perm[0][:, None] == jnp.arange(slots)[None, :]
    ordered = jnp.sum(
        jnp.where(hits[:, :, None, None, None], pooled[None], jnp.zeros_like(pooled[None])), axis=1
    )
    part = channel_map(u_pool, ordered)
    pre = exchange_sum(part, coarse_state.shape[0])
    pre = pre + channel_map(u_state, coarse_state)
    pre = pre + b_coarse[None, :, None, None]
    coarse_next = coarse_state + jnp.tanh(pre)
    return (new_half, coarse_next)


def solution(mesh):
    return jax.shard_map(
        shards,
        mesh=mesh,
        in_specs=(
            P(("groups", "band"), "tiles", None, None, None),
            P(("groups", "band"), "tiles", None, None, None),
            P("tiles"),
            P("tiles", None),
            P("tiles", None),
            P(("groups", "tiles", "band"), None, None, None),
            P(),
            P(),
            P(),
            P(),
            P(),
            P(),
            P(),
            P(),
            P(),
        ),
        out_specs=(
            P(("groups", "band"), "tiles", "rep", None, None),
            P(("groups", "tiles", "band"), None, None, None),
        ),
        check_vma=False,
    )
```

```python
import jax
import jax.numpy as jnp
from jax import lax
from jax.sharding import PartitionSpec as P


def padded(block, sides, width):
    for axis, dim in sides:
        count = lax.axis_size(axis)
        forward = [(i, i + 1) for i in range(count - 1)]
        backward = [(target, source) for source, target in forward]
        low = lax.ppermute(
            lax.slice_in_dim(block, block.shape[dim] - width, None, axis=dim), axis, forward
        )
        high = lax.ppermute(lax.slice_in_dim(block, 0, width, axis=dim), axis, backward)
        block = jnp.concatenate([low, block, high], axis=dim)
    return block


def apply_filter(
    padded_input, filter_weight, dilation_rate, first_row_index, row_count, column_count
):
    total = None
    for left_operand in (-1, 0, 1):
        for right_operand in (-1, 0, 1):
            window_slice = padded_input[
                :,
                :,
                :,
                first_row_index
                + left_operand * dilation_rate : first_row_index
                + left_operand * dilation_rate
                + row_count,
                2
                + right_operand * dilation_rate : 2
                + right_operand * dilation_rate
                + column_count,
            ]
            term = jnp.einsum(
                "oi,bsirw->bsorw",
                filter_weight[(left_operand + 1) * 3 + (right_operand + 1)],
                window_slice,
                preferred_element_type=jnp.float32,
            )
            total = term if total is None else total + term
    return total


def choose_rows(block, select):
    masked = jnp.where(select[None, :, None, None, None], block, jnp.zeros_like(block))
    return jnp.sum(masked, axis=1)


def logistic(value):
    return 0.5 + 0.5 * jnp.tanh(0.5 * value)


def exchange_sum(part, owned):
    bands = lax.axis_size("band")
    reps = lax.axis_size("rep")
    band = lax.axis_index("band")
    total = None
    for shift in range(bands):
        pair = None
        for step in range(reps):
            target = (band + shift) % bands
            chunk = lax.dynamic_slice_in_dim(part, target * owned, owned, 0)
            if shift or step:
                perm = [
                    (b * reps + r, ((b + shift) % bands) * reps + (r + step) % reps)
                    for b in range(bands)
                    for r in range(reps)
                ]
                chunk = lax.ppermute(chunk, ("band", "rep"), perm)
            pair = chunk if pair is None else pair + chunk
        total = pair if total is None else total + pair
    return total


def shards(
    features,
    state,
    live,
    neighbours,
    coarse_perm,
    coarse_state,
    w_update,
    b_update,
    w_reset,
    b_reset,
    w_cand,
    b_cand,
    u_pool,
    u_state,
    b_coarse,
):
    reps = lax.axis_size("rep")
    rep = lax.axis_index("rep")
    per_core = features.shape[0] // reps
    features = lax.dynamic_slice_in_dim(features, rep * per_core, per_core, 0)
    state = lax.dynamic_slice_in_dim(state, rep * per_core, per_core, 0)
    slots = state.shape[1]
    chans = state.shape[2]
    row_count = state.shape[3]
    column_count = state.shape[4]
    inputs_count = features.shape[2]
    half = chans // lax.axis_size("rep")
    start = lax.axis_index("rep") * half
    base = lax.axis_index("tiles") * slots
    ups = neighbours[:, 0]
    downs = neighbours[:, 1]
    up_here = (ups >= base) & (ups < base + slots)
    down_here = (downs >= base) & (downs < base + slots)
    up_far = (ups >= 0) & jnp.logical_not(up_here)
    down_far = (downs >= 0) & jnp.logical_not(down_here)
    alive = live > 0
    first_sel = alive & jnp.logical_not(up_here)
    last_sel = alive & jnp.logical_not(down_here)

    def own_out(filter_weight):
        return lax.dynamic_slice_in_dim(filter_weight, start, half, 1)

    def own_bias(bias):
        return lax.dynamic_slice_in_dim(bias, start, half, 0)[:, None, None]

    hb = state.astype(jnp.bfloat16)
    joined = jnp.concatenate([features, hb], axis=2)
    top = choose_rows(joined[:, :, :, :3, :], first_sel)
    bottom = choose_rows(joined[:, :, :, row_count - 3 :, :], last_sel)
    cycle = padded(jnp.concatenate([top, bottom], axis=2), (("tiles", 2),), 3)
    cycle_prev = cycle[:, None, :, :3, :]
    cycle_next = cycle[:, None, :, 3 * 3 : 4 * 3, :]
    top_local = jnp.take(
        joined[:, :, :, row_count - 3 :, :], jnp.clip(ups - base, 0, slots - 1), axis=1
    )
    bottom_local = jnp.take(joined[:, :, :, :3, :], jnp.clip(downs - base, 0, slots - 1), axis=1)
    zeros_rows = jnp.zeros_like(top_local)
    top = jnp.where(
        up_here[None, :, None, None, None],
        top_local,
        jnp.where(up_far[None, :, None, None, None], cycle_prev + zeros_rows, zeros_rows),
    )
    bottom = jnp.where(
        down_here[None, :, None, None, None],
        bottom_local,
        jnp.where(down_far[None, :, None, None, None], cycle_next + zeros_rows, zeros_rows),
    )
    full = jnp.concatenate([top, joined, bottom], axis=3)
    first = jnp.pad(full, ((0, 0), (0, 0), (0, 0), (0, 0), (2, 2)))
    gates = logistic(
        apply_filter(
            first,
            jnp.concatenate([w_update, w_reset], axis=1),
            1,
            1,
            row_count + 4,
            column_count,
        )
        + jnp.concatenate([b_update, b_reset])[:, None, None]
    )
    update = gates[:, :, :chans, 2 : row_count + 2]
    reset = gates[:, :, chans:]
    hidden_wide = first[:, :, inputs_count:, 1 : row_count + 5, 2 : column_count + 2]
    gated = (reset * hidden_wide.astype(jnp.float32)).astype(jnp.bfloat16)
    gated_pad = jnp.pad(gated, ((0, 0), (0, 0), (0, 0), (0, 0), (2, 2)))
    second = jnp.concatenate([first[:, :, :inputs_count, 1 : row_count + 5, :], gated_pad], axis=2)
    candidate = jnp.tanh(
        apply_filter(second, w_cand, 2, 2, row_count, column_count) + b_cand[:, None, None]
    )
    live_scale = alive.astype(jnp.float32)[None, :, None, None, None]
    new_state = ((1.0 - update) * state + update * candidate) * live_scale
    groups = []
    for step in range(reps):
        piece = lax.dynamic_slice_in_dim(new_state, ((rep + step) % reps) * half, half, 2)
        if step:
            piece = lax.ppermute(piece, "rep", [(r, (r + step) % reps) for r in range(reps)])
        groups.append(piece)
    new_half = jnp.concatenate(
        [
            sum(
                jnp.where((rep - step) % reps == owner, piece, jnp.zeros_like(piece))
                for step, piece in enumerate(groups)
            )
            for owner in range(reps)
        ],
        axis=0,
    )
    summed = jnp.sum(new_state, axis=0)
    column_pool = (
        jnp.arange(column_count)[:, None] // 4 == jnp.arange(column_count // 4)[None, :]
    ).astype(jnp.float32)
    cols = jnp.einsum(
        "schw,wj->schj", summed, column_pool, precision=lax.Precision.HIGHEST
    )
    pooled = jnp.sum(
        cols.reshape(slots, chans, row_count // 4, 4, column_count // 4), axis=3
    ) / 16.0
    ordered = jnp.take(pooled, coarse_perm[0], axis=0)
    part = jnp.einsum("oc,kcij->koij", u_pool, ordered, precision=lax.Precision.HIGHEST)
    pre = exchange_sum(part, coarse_state.shape[0])
    pre = pre + jnp.einsum("oc,kcij->koij", u_state, coarse_state, precision=lax.Precision.HIGHEST)
    pre = pre + b_coarse[None, :, None, None]
    coarse_next = coarse_state + jnp.tanh(pre)
    return (new_half, coarse_next)


def solution(mesh):
    return jax.shard_map(
        shards,
        mesh=mesh,
        in_specs=(
            P(("groups", "band"), "tiles", None, None, None),
            P(("groups", "band"), "tiles", None, None, None),
            P("tiles"),
            P("tiles", None),
            P("tiles", None),
            P(("groups", "tiles", "band"), None, None, None),
            P(),
            P(),
            P(),
            P(),
            P(),
            P(),
            P(),
            P(),
            P(),
        ),
        out_specs=(
            P(("groups", "band"), "tiles", "rep", None, None),
            P(("groups", "tiles", "band"), None, None, None),
        ),
        check_vma=False,
    )
```

```python
import jax
import jax.numpy as jnp
from jax import lax
from jax.sharding import PartitionSpec as P


def padded(block, sides, width):
    for axis, dim in sides:
        count = lax.axis_size(axis)
        forward = [(i, i + 1) for i in range(count - 1)]
        backward = [(target, source) for source, target in forward]
        low = lax.ppermute(
            lax.slice_in_dim(block, block.shape[dim] - width, None, axis=dim), axis, forward
        )
        high = lax.ppermute(lax.slice_in_dim(block, 0, width, axis=dim), axis, backward)
        block = jnp.concatenate([low, block, high], axis=dim)
    return block


def apply_filter(
    padded_input, filter_weight, dilation_rate, first_row_index, row_count, column_count
):
    total = None
    for left_operand in (-1, 0, 1):
        for right_operand in (-1, 0, 1):
            window_slice = padded_input[
                :,
                :,
                :,
                first_row_index
                + left_operand * dilation_rate : first_row_index
                + left_operand * dilation_rate
                + row_count,
                2
                + right_operand * dilation_rate : 2
                + right_operand * dilation_rate
                + column_count,
            ]
            term = jnp.einsum(
                "oi,bsirw->bsorw",
                filter_weight[(left_operand + 1) * 3 + (right_operand + 1)],
                window_slice,
                preferred_element_type=jnp.float32,
            )
            total = term if total is None else total + term
    return total


def choose_rows(block, select):
    masked = jnp.where(select[None, :, None, None, None], block, jnp.zeros_like(block))
    return jnp.sum(masked, axis=1)


def logistic(value):
    return 0.5 + 0.5 * jnp.tanh(0.5 * value)


def rep_sum(part):
    reps = lax.axis_size("rep")
    total = part
    for step in range(1, reps):
        total = total + lax.ppermute(part, "rep", [(r, (r + step) % reps) for r in range(reps)])
    return total


def exchange_sum(part, owned):
    bands = lax.axis_size("band")
    band = lax.axis_index("band")
    total = None
    for shift in range(bands):
        target = (band + shift) % bands
        chunk = lax.dynamic_slice_in_dim(part, target * owned, owned, 0)
        if shift:
            perm = [(b, (b + shift) % bands) for b in range(bands)]
            chunk = lax.ppermute(chunk, "band", perm)
        total = chunk if total is None else total + chunk
    return total


def shards(
    features,
    state,
    live,
    neighbours,
    coarse_perm,
    coarse_state,
    w_update,
    b_update,
    w_reset,
    b_reset,
    w_cand,
    b_cand,
    u_pool,
    u_state,
    b_coarse,
):
    reps = lax.axis_size("rep")
    rep = lax.axis_index("rep")
    per_core = features.shape[0] // reps
    features = lax.dynamic_slice_in_dim(features, rep * per_core, per_core, 0)
    state = lax.dynamic_slice_in_dim(state, rep * per_core, per_core, 0)
    slots = state.shape[1]
    chans = state.shape[2]
    row_count = state.shape[3]
    column_count = state.shape[4]
    inputs_count = features.shape[2]
    half = chans // lax.axis_size("rep")
    start = lax.axis_index("rep") * half
    base = lax.axis_index("tiles") * slots
    ups = neighbours[:, 0]
    downs = neighbours[:, 1]
    up_here = (ups >= base) & (ups < base + slots)
    down_here = (downs >= base) & (downs < base + slots)
    up_far = (ups >= 0) & jnp.logical_not(up_here)
    down_far = (downs >= 0) & jnp.logical_not(down_here)
    alive = live > 0
    first_sel = alive & jnp.logical_not(up_here)
    last_sel = alive & jnp.logical_not(down_here)

    def own_out(filter_weight):
        return lax.dynamic_slice_in_dim(filter_weight, start, half, 1)

    def own_bias(bias):
        return lax.dynamic_slice_in_dim(bias, start, half, 0)[:, None, None]

    hb = state.astype(jnp.bfloat16)
    joined = jnp.concatenate([features, hb], axis=2)
    top = choose_rows(joined[:, :, :, :3, :], first_sel)
    bottom = choose_rows(joined[:, :, :, row_count - 3 :, :], last_sel)
    cycle = padded(jnp.concatenate([top, bottom], axis=2), (("tiles", 2),), 3)
    cycle_prev = cycle[:, None, :, :3, :]
    cycle_next = cycle[:, None, :, 3 * 3 : 4 * 3, :]
    top_local = jnp.take(
        joined[:, :, :, row_count - 3 :, :], jnp.clip(ups - base, 0, slots - 1), axis=1
    )
    bottom_local = jnp.take(joined[:, :, :, :3, :], jnp.clip(downs - base, 0, slots - 1), axis=1)
    zeros_rows = jnp.zeros_like(top_local)
    top = jnp.where(
        up_here[None, :, None, None, None],
        top_local,
        jnp.where(up_far[None, :, None, None, None], cycle_prev + zeros_rows, zeros_rows),
    )
    bottom = jnp.where(
        down_here[None, :, None, None, None],
        bottom_local,
        jnp.where(down_far[None, :, None, None, None], cycle_next + zeros_rows, zeros_rows),
    )
    full = jnp.concatenate([top, joined, bottom], axis=3)
    first = jnp.pad(full, ((0, 0), (0, 0), (0, 0), (0, 0), (2, 2)))
    gates = logistic(
        apply_filter(
            first,
            jnp.concatenate([w_update, w_reset], axis=1),
            1,
            1,
            row_count + 4,
            column_count,
        )
        + jnp.concatenate([b_update, b_reset])[:, None, None]
    )
    update = gates[:, :, :chans, 2 : row_count + 2]
    reset = gates[:, :, chans:]
    hidden_wide = first[:, :, inputs_count:, 1 : row_count + 5, 2 : column_count + 2]
    gated = (reset * hidden_wide.astype(jnp.float32)).astype(jnp.bfloat16)
    gated_pad = jnp.pad(gated, ((0, 0), (0, 0), (0, 0), (0, 0), (2, 2)))
    second = jnp.concatenate([first[:, :, :inputs_count, 1 : row_count + 5, :], gated_pad], axis=2)
    candidate = jnp.tanh(
        apply_filter(second, w_cand, 2, 2, row_count, column_count) + b_cand[:, None, None]
    )
    live_scale = alive.astype(jnp.float32)[None, :, None, None, None]
    new_state = ((1.0 - update) * state + update * candidate) * live_scale
    groups = []
    for step in range(reps):
        piece = lax.dynamic_slice_in_dim(new_state, ((rep + step) % reps) * half, half, 2)
        if step:
            piece = lax.ppermute(piece, "rep", [(r, (r + step) % reps) for r in range(reps)])
        groups.append(piece)
    new_half = jnp.concatenate(
        [
            sum(
                jnp.where((rep - step) % reps == owner, piece, jnp.zeros_like(piece))
                for step, piece in enumerate(groups)
            )
            for owner in range(reps)
        ],
        axis=0,
    )
    summed = jnp.sum(new_state, axis=0)
    column_pool = (
        jnp.arange(column_count)[:, None] // 4 == jnp.arange(column_count // 4)[None, :]
    ).astype(jnp.float32)
    cols = jnp.einsum(
        "schw,wj->schj", summed, column_pool, precision=lax.Precision.HIGHEST
    )
    pooled = jnp.sum(
        cols.reshape(slots, chans, row_count // 4, 4, column_count // 4), axis=3
    ) / 16.0
    ordered = jnp.take(pooled, coarse_perm[0], axis=0)
    part = jnp.einsum("oc,kcij->koij", u_pool, ordered, precision=lax.Precision.HIGHEST)
    pre = exchange_sum(rep_sum(part), coarse_state.shape[0])
    pre = pre + jnp.einsum("oc,kcij->koij", u_state, coarse_state, precision=lax.Precision.HIGHEST)
    pre = pre + b_coarse[None, :, None, None]
    coarse_next = coarse_state + jnp.tanh(pre)
    return (new_half, coarse_next)


def solution(mesh):
    return jax.shard_map(
        shards,
        mesh=mesh,
        in_specs=(
            P(("groups", "band"), "tiles", None, None, None),
            P(("groups", "band"), "tiles", None, None, None),
            P("tiles"),
            P("tiles", None),
            P("tiles", None),
            P(("groups", "tiles", "band"), None, None, None),
            P(),
            P(),
            P(),
            P(),
            P(),
            P(),
            P(),
            P(),
            P(),
        ),
        out_specs=(
            P(("groups", "band"), "tiles", "rep", None, None),
            P(("groups", "tiles", "band"), None, None, None),
        ),
        check_vma=False,
    )
```

```python
import jax
import jax.numpy as jnp
from jax import lax
from jax.sharding import PartitionSpec as P


def padded(block, sides, width):
    for axis, dim in sides:
        count = lax.axis_size(axis)
        forward = [(i, i + 1) for i in range(count - 1)]
        backward = [(target, source) for source, target in forward]
        low = lax.ppermute(
            lax.slice_in_dim(block, block.shape[dim] - width, None, axis=dim), axis, forward
        )
        high = lax.ppermute(lax.slice_in_dim(block, 0, width, axis=dim), axis, backward)
        block = jnp.concatenate([low, block, high], axis=dim)
    return block


def apply_filter(
    padded_input, filter_weight, dilation_rate, first_row_index, row_count, column_count
):
    total = None
    for left_operand in (-1, 0, 1):
        for right_operand in (-1, 0, 1):
            window_slice = padded_input[
                :,
                :,
                :,
                first_row_index
                + left_operand * dilation_rate : first_row_index
                + left_operand * dilation_rate
                + row_count,
                2
                + right_operand * dilation_rate : 2
                + right_operand * dilation_rate
                + column_count,
            ]
            term = jnp.einsum(
                "oi,bsirw->bsorw",
                filter_weight[(left_operand + 1) * 3 + (right_operand + 1)],
                window_slice,
                preferred_element_type=jnp.float32,
            )
            total = term if total is None else total + term
    return total


def choose_rows(block, select):
    masked = jnp.where(select[None, :, None, None, None], block, jnp.zeros_like(block))
    return jnp.sum(masked, axis=1)


def logistic(value):
    return 0.5 + 0.5 * jnp.tanh(0.5 * value)


def rep_sum(part):
    reps = lax.axis_size("rep")
    total = part
    for step in range(1, reps):
        total = total + lax.ppermute(part, "rep", [(r, (r + step) % reps) for r in range(reps)])
    return total


def exchange_sum(part, owned):
    bands = lax.axis_size("band")
    band = lax.axis_index("band")
    total = None
    for shift in range(bands):
        target = (band + shift) % bands
        chunk = lax.dynamic_slice_in_dim(part, target * owned, owned, 0)
        if shift:
            perm = [(b, (b + shift) % bands) for b in range(bands)]
            chunk = lax.ppermute(chunk, "band", perm)
        total = chunk if total is None else total + chunk
    return total


def shards(
    features,
    state,
    live,
    neighbours,
    coarse_perm,
    coarse_state,
    w_update,
    b_update,
    w_reset,
    b_reset,
    w_cand,
    b_cand,
    u_pool,
    u_state,
    b_coarse,
):
    reps = lax.axis_size("rep")
    rep = lax.axis_index("rep")
    per_core = features.shape[0] // reps
    features = lax.dynamic_slice_in_dim(features, rep * per_core, per_core, 0)
    state = lax.dynamic_slice_in_dim(state, rep * per_core, per_core, 0)
    slots = state.shape[1]
    chans = state.shape[2]
    row_count = state.shape[3]
    column_count = state.shape[4]
    inputs_count = features.shape[2]
    half = chans // lax.axis_size("rep")
    start = lax.axis_index("rep") * half
    base = lax.axis_index("tiles") * slots
    ups = neighbours[:, 0]
    downs = neighbours[:, 1]
    up_here = (ups >= base) & (ups < base + slots)
    down_here = (downs >= base) & (downs < base + slots)
    up_far = (ups >= 0) & jnp.logical_not(up_here)
    down_far = (downs >= 0) & jnp.logical_not(down_here)
    alive = live > 0
    first_sel = alive & jnp.logical_not(up_here)
    last_sel = alive & jnp.logical_not(down_here)

    def own_out(filter_weight):
        return lax.dynamic_slice_in_dim(filter_weight, start, half, 1)

    def own_bias(bias):
        return lax.dynamic_slice_in_dim(bias, start, half, 0)[:, None, None]

    hb = state.astype(jnp.bfloat16)
    joined = jnp.concatenate([features, hb], axis=2)
    top = choose_rows(joined[:, :, :, :3, :], first_sel)
    bottom = choose_rows(joined[:, :, :, row_count - 3 :, :], last_sel)
    cycle = padded(jnp.concatenate([top, bottom], axis=2), (("tiles", 2),), 3)
    cycle_prev = cycle[:, None, :, :3, :]
    cycle_next = cycle[:, None, :, 3 * 3 : 4 * 3, :]
    top_local = jnp.take(
        joined[:, :, :, row_count - 3 :, :], jnp.clip(ups - base, 0, slots - 1), axis=1
    )
    bottom_local = jnp.take(joined[:, :, :, :3, :], jnp.clip(downs - base, 0, slots - 1), axis=1)
    zeros_rows = jnp.zeros_like(top_local)
    top = jnp.where(
        up_here[None, :, None, None, None],
        top_local,
        jnp.where(up_far[None, :, None, None, None], cycle_prev + zeros_rows, zeros_rows),
    )
    bottom = jnp.where(
        down_here[None, :, None, None, None],
        bottom_local,
        jnp.where(down_far[None, :, None, None, None], cycle_next + zeros_rows, zeros_rows),
    )
    full = jnp.concatenate([top, joined, bottom], axis=3)
    first = jnp.pad(full, ((0, 0), (0, 0), (0, 0), (0, 0), (2, 2)))
    gates = logistic(
        apply_filter(
            first,
            jnp.concatenate([w_update, w_reset], axis=1),
            1,
            1,
            row_count + 4,
            column_count,
        )
        + jnp.concatenate([b_update, b_reset])[:, None, None]
    )
    update = gates[:, :, :chans, 2 : row_count + 2]
    reset = gates[:, :, chans:]
    hidden_wide = first[:, :, inputs_count:, 1 : row_count + 5, 2 : column_count + 2]
    gated = (reset * hidden_wide.astype(jnp.float32)).astype(jnp.bfloat16)
    gated_pad = jnp.pad(gated, ((0, 0), (0, 0), (0, 0), (0, 0), (2, 2)))
    second = jnp.concatenate([first[:, :, :inputs_count, 1 : row_count + 5, :], gated_pad], axis=2)
    candidate = jnp.tanh(
        apply_filter(second, w_cand, 2, 2, row_count, column_count) + b_cand[:, None, None]
    )
    live_scale = alive.astype(jnp.float32)[None, :, None, None, None]
    new_state = ((1.0 - update) * state + update * candidate) * live_scale
    groups = []
    for step in range(reps):
        piece = lax.dynamic_slice_in_dim(new_state, ((rep + step) % reps) * half, half, 2)
        if step:
            piece = lax.ppermute(piece, "rep", [(r, (r + step) % reps) for r in range(reps)])
        groups.append(piece)
    new_half = jnp.concatenate(
        [
            sum(
                jnp.where((rep - step) % reps == owner, piece, jnp.zeros_like(piece))
                for step, piece in enumerate(groups)
            )
            for owner in range(reps)
        ],
        axis=0,
    )
    summed = jnp.sum(new_state, axis=0)
    column_pool = (
        jnp.arange(column_count)[:, None] // 4 == jnp.arange(column_count // 4)[None, :]
    ).astype(jnp.float32)
    cols = jnp.einsum(
        "schw,wj->schj", summed, column_pool, precision=lax.Precision.HIGHEST
    )
    pooled = jnp.sum(
        cols.reshape(slots, chans, row_count // 4, 4, column_count // 4), axis=3
    ) / 16.0
    ordered = jnp.take(pooled, coarse_perm[0], axis=0)
    part = jnp.einsum("oc,kcij->koij", u_pool, ordered, precision=lax.Precision.HIGHEST)
    new_half, chip_part = lax.optimization_barrier((new_half, rep_sum(part)))
    pre = exchange_sum(chip_part, coarse_state.shape[0])
    pre = pre + jnp.einsum("oc,kcij->koij", u_state, coarse_state, precision=lax.Precision.HIGHEST)
    pre = pre + b_coarse[None, :, None, None]
    coarse_next = coarse_state + jnp.tanh(pre)
    return (new_half, coarse_next)


def solution(mesh):
    return jax.shard_map(
        shards,
        mesh=mesh,
        in_specs=(
            P(("groups", "band"), "tiles", None, None, None),
            P(("groups", "band"), "tiles", None, None, None),
            P("tiles"),
            P("tiles", None),
            P("tiles", None),
            P(("groups", "tiles", "band"), None, None, None),
            P(),
            P(),
            P(),
            P(),
            P(),
            P(),
            P(),
            P(),
            P(),
        ),
        out_specs=(
            P(("groups", "band"), "tiles", "rep", None, None),
            P(("groups", "tiles", "band"), None, None, None),
        ),
        check_vma=False,
    )
```

```python
import jax
import jax.numpy as jnp
from jax import lax
from jax.sharding import PartitionSpec as P


def padded(block, sides, width):
    for axis, dim in sides:
        count = lax.axis_size(axis)
        forward = [(i, i + 1) for i in range(count - 1)]
        backward = [(target, source) for source, target in forward]
        low = lax.ppermute(
            lax.slice_in_dim(block, block.shape[dim] - width, None, axis=dim), axis, forward
        )
        high = lax.ppermute(lax.slice_in_dim(block, 0, width, axis=dim), axis, backward)
        block = jnp.concatenate([low, block, high], axis=dim)
    return block


def apply_filter(
    padded_input, filter_weight, dilation_rate, first_row_index, row_count, column_count
):
    offsets = (-1, 0, 1)
    stacked = jnp.concatenate(
        [
            padded_input[
                :,
                :,
                :,
                first_row_index
                + row_offset * dilation_rate : first_row_index
                + row_offset * dilation_rate
                + row_count,
                :,
            ]
            for row_offset in offsets
        ],
        axis=2,
    )
    total = None
    for column_offset in offsets:
        weight = jnp.concatenate(
            [filter_weight[(row_offset + 1) * 3 + (column_offset + 1)] for row_offset in offsets],
            axis=1,
        )
        window_slice = stacked[
            ...,
            2 + column_offset * dilation_rate : 2 + column_offset * dilation_rate + column_count,
        ]
        term = jnp.einsum(
            "oi,bsirw->bsorw", weight, window_slice, preferred_element_type=jnp.float32
        )
        total = term if total is None else total + term
    return total


def choose_rows(block, select):
    masked = jnp.where(select[None, :, None, None, None], block, jnp.zeros_like(block))
    return jnp.sum(masked, axis=1)


def logistic(value):
    return 0.5 + 0.5 * jnp.tanh(0.5 * value)


def rep_sum(part):
    reps = lax.axis_size("rep")
    total = part
    for step in range(1, reps):
        total = total + lax.ppermute(part, "rep", [(r, (r + step) % reps) for r in range(reps)])
    return total


def exchange_sum(part, owned):
    bands = lax.axis_size("band")
    band = lax.axis_index("band")
    total = None
    for shift in range(bands):
        target = (band + shift) % bands
        chunk = lax.dynamic_slice_in_dim(part, target * owned, owned, 0)
        if shift:
            perm = [(b, (b + shift) % bands) for b in range(bands)]
            chunk = lax.ppermute(chunk, "band", perm)
        total = chunk if total is None else total + chunk
    return total


def shards(
    features,
    state,
    live,
    neighbours,
    coarse_perm,
    coarse_state,
    w_update,
    b_update,
    w_reset,
    b_reset,
    w_cand,
    b_cand,
    u_pool,
    u_state,
    b_coarse,
):
    reps = lax.axis_size("rep")
    rep = lax.axis_index("rep")
    per_core = features.shape[0] // reps
    features = lax.dynamic_slice_in_dim(features, rep * per_core, per_core, 0)
    state = lax.dynamic_slice_in_dim(state, rep * per_core, per_core, 0)
    slots = state.shape[1]
    chans = state.shape[2]
    row_count = state.shape[3]
    column_count = state.shape[4]
    inputs_count = features.shape[2]
    half = chans // lax.axis_size("rep")
    start = lax.axis_index("rep") * half
    base = lax.axis_index("tiles") * slots
    ups = neighbours[:, 0]
    downs = neighbours[:, 1]
    up_here = (ups >= base) & (ups < base + slots)
    down_here = (downs >= base) & (downs < base + slots)
    up_far = (ups >= 0) & jnp.logical_not(up_here)
    down_far = (downs >= 0) & jnp.logical_not(down_here)
    alive = live > 0
    first_sel = alive & jnp.logical_not(up_here)
    last_sel = alive & jnp.logical_not(down_here)

    def own_out(filter_weight):
        return lax.dynamic_slice_in_dim(filter_weight, start, half, 1)

    def own_bias(bias):
        return lax.dynamic_slice_in_dim(bias, start, half, 0)[:, None, None]

    hb = state.astype(jnp.bfloat16)
    joined = jnp.concatenate([features, hb], axis=2)
    top = choose_rows(joined[:, :, :, :3, :], first_sel)
    bottom = choose_rows(joined[:, :, :, row_count - 3 :, :], last_sel)
    cycle = padded(jnp.concatenate([top, bottom], axis=2), (("tiles", 2),), 3)
    cycle_prev = cycle[:, None, :, :3, :]
    cycle_next = cycle[:, None, :, 3 * 3 : 4 * 3, :]
    top_local = jnp.take(
        joined[:, :, :, row_count - 3 :, :], jnp.clip(ups - base, 0, slots - 1), axis=1
    )
    bottom_local = jnp.take(joined[:, :, :, :3, :], jnp.clip(downs - base, 0, slots - 1), axis=1)
    zeros_rows = jnp.zeros_like(top_local)
    top = jnp.where(
        up_here[None, :, None, None, None],
        top_local,
        jnp.where(up_far[None, :, None, None, None], cycle_prev + zeros_rows, zeros_rows),
    )
    bottom = jnp.where(
        down_here[None, :, None, None, None],
        bottom_local,
        jnp.where(down_far[None, :, None, None, None], cycle_next + zeros_rows, zeros_rows),
    )
    full = jnp.concatenate([top, joined, bottom], axis=3)
    first = jnp.pad(full, ((0, 0), (0, 0), (0, 0), (0, 0), (2, 2)))
    gates = logistic(
        apply_filter(
            first,
            jnp.concatenate([w_update, w_reset], axis=1),
            1,
            1,
            row_count + 4,
            column_count,
        )
        + jnp.concatenate([b_update, b_reset])[:, None, None]
    )
    update = gates[:, :, :chans, 2 : row_count + 2]
    reset = gates[:, :, chans:]
    hidden_wide = first[:, :, inputs_count:, 1 : row_count + 5, 2 : column_count + 2]
    gated = (reset * hidden_wide.astype(jnp.float32)).astype(jnp.bfloat16)
    gated_pad = jnp.pad(gated, ((0, 0), (0, 0), (0, 0), (0, 0), (2, 2)))
    second = jnp.concatenate([first[:, :, :inputs_count, 1 : row_count + 5, :], gated_pad], axis=2)
    candidate = jnp.tanh(
        apply_filter(second, w_cand, 2, 2, row_count, column_count) + b_cand[:, None, None]
    )
    live_scale = alive.astype(jnp.float32)[None, :, None, None, None]
    new_state = ((1.0 - update) * state + update * candidate) * live_scale
    groups = []
    for step in range(reps):
        piece = lax.dynamic_slice_in_dim(new_state, ((rep + step) % reps) * half, half, 2)
        if step:
            piece = lax.ppermute(piece, "rep", [(r, (r + step) % reps) for r in range(reps)])
        groups.append(piece)
    new_half = jnp.concatenate(
        [
            sum(
                jnp.where((rep - step) % reps == owner, piece, jnp.zeros_like(piece))
                for step, piece in enumerate(groups)
            )
            for owner in range(reps)
        ],
        axis=0,
    )
    summed = jnp.sum(new_state, axis=0)
    column_pool = (
        jnp.arange(column_count)[:, None] // 4 == jnp.arange(column_count // 4)[None, :]
    ).astype(jnp.float32)
    cols = jnp.einsum(
        "schw,wj->schj", summed, column_pool, precision=lax.Precision.HIGHEST
    )
    pooled = jnp.sum(
        cols.reshape(slots, chans, row_count // 4, 4, column_count // 4), axis=3
    ) / 16.0
    ordered = jnp.take(pooled, coarse_perm[0], axis=0)
    part = jnp.einsum("oc,kcij->koij", u_pool, ordered, precision=lax.Precision.HIGHEST)
    new_half, chip_part = lax.optimization_barrier((new_half, rep_sum(part)))
    pre = exchange_sum(chip_part, coarse_state.shape[0])
    pre = pre + jnp.einsum("oc,kcij->koij", u_state, coarse_state, precision=lax.Precision.HIGHEST)
    pre = pre + b_coarse[None, :, None, None]
    coarse_next = coarse_state + jnp.tanh(pre)
    return (new_half, coarse_next)


def solution(mesh):
    return jax.shard_map(
        shards,
        mesh=mesh,
        in_specs=(
            P(("groups", "band"), "tiles", None, None, None),
            P(("groups", "band"), "tiles", None, None, None),
            P("tiles"),
            P("tiles", None),
            P("tiles", None),
            P(("groups", "tiles", "band"), None, None, None),
            P(),
            P(),
            P(),
            P(),
            P(),
            P(),
            P(),
            P(),
            P(),
        ),
        out_specs=(
            P(("groups", "band"), "tiles", "rep", None, None),
            P(("groups", "tiles", "band"), None, None, None),
        ),
        check_vma=False,
    )
```

```python
import jax
import jax.numpy as jnp
from jax import lax
from jax.sharding import PartitionSpec as P


def padded(block, sides, width):
    for axis, dim in sides:
        count = lax.axis_size(axis)
        forward = [(i, i + 1) for i in range(count - 1)]
        backward = [(target, source) for source, target in forward]
        low = lax.ppermute(
            lax.slice_in_dim(block, block.shape[dim] - width, None, axis=dim), axis, forward
        )
        high = lax.ppermute(lax.slice_in_dim(block, 0, width, axis=dim), axis, backward)
        block = jnp.concatenate([low, block, high], axis=dim)
    return block


def row_stack(padded_input, dilation_rate, first_row_index, row_count):
    return jnp.concatenate(
        [
            padded_input[
                :,
                :,
                :,
                first_row_index
                + row_offset * dilation_rate : first_row_index
                + row_offset * dilation_rate
                + row_count,
                :,
            ]
            for row_offset in (-1, 0, 1)
        ],
        axis=2,
    )


def apply_stacked(stacked, filter_weight, dilation_rate, column_count):
    offsets = (-1, 0, 1)
    total = None
    for column_offset in offsets:
        weight = jnp.concatenate(
            [filter_weight[(row_offset + 1) * 3 + (column_offset + 1)] for row_offset in offsets],
            axis=1,
        )
        window_slice = stacked[
            ...,
            2 + column_offset * dilation_rate : 2 + column_offset * dilation_rate + column_count,
        ]
        term = jnp.einsum(
            "oi,bsirw->bsorw", weight, window_slice, preferred_element_type=jnp.float32
        )
        total = term if total is None else total + term
    return total


def apply_filter(
    padded_input, filter_weight, dilation_rate, first_row_index, row_count, column_count
):
    stacked = row_stack(padded_input, dilation_rate, first_row_index, row_count)
    return apply_stacked(stacked, filter_weight, dilation_rate, column_count)


def choose_rows(block, select):
    masked = jnp.where(select[None, :, None, None, None], block, jnp.zeros_like(block))
    return jnp.sum(masked, axis=1)


def logistic(value):
    return 0.5 + 0.5 * jnp.tanh(0.5 * value)


def rep_sum(part):
    reps = lax.axis_size("rep")
    total = part
    for step in range(1, reps):
        total = total + lax.ppermute(part, "rep", [(r, (r + step) % reps) for r in range(reps)])
    return total


def exchange_sum(part, owned):
    bands = lax.axis_size("band")
    band = lax.axis_index("band")
    total = None
    for shift in range(bands):
        target = (band + shift) % bands
        chunk = lax.dynamic_slice_in_dim(part, target * owned, owned, 0)
        if shift:
            perm = [(b, (b + shift) % bands) for b in range(bands)]
            chunk = lax.ppermute(chunk, "band", perm)
        total = chunk if total is None else total + chunk
    return total


def shards(
    features,
    state,
    live,
    neighbours,
    coarse_perm,
    coarse_state,
    w_update,
    b_update,
    w_reset,
    b_reset,
    w_cand,
    b_cand,
    u_pool,
    u_state,
    b_coarse,
):
    reps = lax.axis_size("rep")
    rep = lax.axis_index("rep")
    per_core = features.shape[0] // reps
    features = lax.dynamic_slice_in_dim(features, rep * per_core, per_core, 0)
    state = lax.dynamic_slice_in_dim(state, rep * per_core, per_core, 0)
    slots = state.shape[1]
    chans = state.shape[2]
    row_count = state.shape[3]
    column_count = state.shape[4]
    inputs_count = features.shape[2]
    half = chans // lax.axis_size("rep")
    start = lax.axis_index("rep") * half
    base = lax.axis_index("tiles") * slots
    ups = neighbours[:, 0]
    downs = neighbours[:, 1]
    up_here = (ups >= base) & (ups < base + slots)
    down_here = (downs >= base) & (downs < base + slots)
    up_far = (ups >= 0) & jnp.logical_not(up_here)
    down_far = (downs >= 0) & jnp.logical_not(down_here)
    alive = live > 0
    first_sel = alive & jnp.logical_not(up_here)
    last_sel = alive & jnp.logical_not(down_here)

    def own_out(filter_weight):
        return lax.dynamic_slice_in_dim(filter_weight, start, half, 1)

    def own_bias(bias):
        return lax.dynamic_slice_in_dim(bias, start, half, 0)[:, None, None]

    hb = state.astype(jnp.bfloat16)
    joined = jnp.concatenate([features, hb], axis=2)
    top = choose_rows(joined[:, :, :, :3, :], first_sel)
    bottom = choose_rows(joined[:, :, :, row_count - 3 :, :], last_sel)
    cycle = padded(jnp.concatenate([top, bottom], axis=2), (("tiles", 2),), 3)
    cycle_prev = cycle[:, None, :, :3, :]
    cycle_next = cycle[:, None, :, 3 * 3 : 4 * 3, :]
    top_local = jnp.take(
        joined[:, :, :, row_count - 3 :, :], jnp.clip(ups - base, 0, slots - 1), axis=1
    )
    bottom_local = jnp.take(joined[:, :, :, :3, :], jnp.clip(downs - base, 0, slots - 1), axis=1)
    zeros_rows = jnp.zeros_like(top_local)
    top = jnp.where(
        up_here[None, :, None, None, None],
        top_local,
        jnp.where(up_far[None, :, None, None, None], cycle_prev + zeros_rows, zeros_rows),
    )
    bottom = jnp.where(
        down_here[None, :, None, None, None],
        bottom_local,
        jnp.where(down_far[None, :, None, None, None], cycle_next + zeros_rows, zeros_rows),
    )
    full = jnp.concatenate([top, joined, bottom], axis=3)
    first = jnp.pad(full, ((0, 0), (0, 0), (0, 0), (0, 0), (2, 2)))
    cols_pad = ((0, 0), (0, 0), (0, 0), (0, 0), (2, 2))
    stacked = row_stack(
        jnp.pad(joined, ((0, 0), (0, 0), (0, 0), (3, 3), (2, 2))), 1, 1, row_count + 4
    )
    edge_top = jnp.pad(jnp.concatenate([top, joined[:, :, :, :2]], axis=3), cols_pad)
    edge_bottom = jnp.pad(
        jnp.concatenate([joined[:, :, :, row_count - 2 :], bottom], axis=3), cols_pad
    )
    stacked = stacked.at[:, :, :, :3].set(row_stack(edge_top, 1, 1, 3))
    stacked = stacked.at[:, :, :, row_count + 1 :].set(row_stack(edge_bottom, 1, 1, 3))
    gates = logistic(
        apply_stacked(stacked, jnp.concatenate([w_update, w_reset], axis=1), 1, column_count)
        + jnp.concatenate([b_update, b_reset])[:, None, None]
    )
    update = gates[:, :, :chans, 2 : row_count + 2]
    reset = gates[:, :, chans:]
    hidden_wide = first[:, :, inputs_count:, 1 : row_count + 5, 2 : column_count + 2]
    gated = (reset * hidden_wide.astype(jnp.float32)).astype(jnp.bfloat16)
    gated_pad = jnp.pad(gated, ((0, 0), (0, 0), (0, 0), (0, 0), (2, 2)))
    second = jnp.concatenate([first[:, :, :inputs_count, 1 : row_count + 5, :], gated_pad], axis=2)
    candidate = jnp.tanh(
        apply_filter(second, w_cand, 2, 2, row_count, column_count) + b_cand[:, None, None]
    )
    live_scale = alive.astype(jnp.float32)[None, :, None, None, None]
    new_state = ((1.0 - update) * state + update * candidate) * live_scale
    groups = []
    for step in range(reps):
        piece = lax.dynamic_slice_in_dim(new_state, ((rep + step) % reps) * half, half, 2)
        if step:
            piece = lax.ppermute(piece, "rep", [(r, (r + step) % reps) for r in range(reps)])
        groups.append(piece)
    new_half = jnp.concatenate(
        [
            sum(
                jnp.where((rep - step) % reps == owner, piece, jnp.zeros_like(piece))
                for step, piece in enumerate(groups)
            )
            for owner in range(reps)
        ],
        axis=0,
    )
    summed = jnp.sum(new_state, axis=0)
    column_pool = (
        jnp.arange(column_count)[:, None] // 4 == jnp.arange(column_count // 4)[None, :]
    ).astype(jnp.float32)
    cols = jnp.einsum(
        "schw,wj->schj", summed, column_pool, precision=lax.Precision.HIGHEST
    )
    pooled = jnp.sum(
        cols.reshape(slots, chans, row_count // 4, 4, column_count // 4), axis=3
    ) / 16.0
    ordered = jnp.take(pooled, coarse_perm[0], axis=0)
    part = jnp.einsum("oc,kcij->koij", u_pool, ordered, precision=lax.Precision.HIGHEST)
    new_half, chip_part = lax.optimization_barrier((new_half, rep_sum(part)))
    pre = exchange_sum(chip_part, coarse_state.shape[0])
    pre = pre + jnp.einsum("oc,kcij->koij", u_state, coarse_state, precision=lax.Precision.HIGHEST)
    pre = pre + b_coarse[None, :, None, None]
    coarse_next = coarse_state + jnp.tanh(pre)
    return (new_half, coarse_next)


def solution(mesh):
    return jax.shard_map(
        shards,
        mesh=mesh,
        in_specs=(
            P(("groups", "band"), "tiles", None, None, None),
            P(("groups", "band"), "tiles", None, None, None),
            P("tiles"),
            P("tiles", None),
            P("tiles", None),
            P(("groups", "tiles", "band"), None, None, None),
            P(),
            P(),
            P(),
            P(),
            P(),
            P(),
            P(),
            P(),
            P(),
        ),
        out_specs=(
            P(("groups", "band"), "tiles", "rep", None, None),
            P(("groups", "tiles", "band"), None, None, None),
        ),
        check_vma=False,
    )
```

```python
import jax
import jax.numpy as jnp
from jax import lax
from jax.sharding import PartitionSpec as P


def padded(block, sides, width):
    for axis, dim in sides:
        count = lax.axis_size(axis)
        forward = [(i, i + 1) for i in range(count - 1)]
        backward = [(target, source) for source, target in forward]
        low = lax.ppermute(
            lax.slice_in_dim(block, block.shape[dim] - width, None, axis=dim), axis, forward
        )
        high = lax.ppermute(lax.slice_in_dim(block, 0, width, axis=dim), axis, backward)
        block = jnp.concatenate([low, block, high], axis=dim)
    return block


def apply_filter(
    padded_input, filter_weight, dilation_rate, first_row_index, row_count, column_count
):
    offsets = (-1, 0, 1)
    stacked = jnp.concatenate(
        [
            padded_input[
                :,
                :,
                :,
                first_row_index
                + row_offset * dilation_rate : first_row_index
                + row_offset * dilation_rate
                + row_count,
                :,
            ]
            for row_offset in offsets
        ],
        axis=2,
    )
    total = None
    for column_offset in offsets:
        weight = jnp.concatenate(
            [filter_weight[(row_offset + 1) * 3 + (column_offset + 1)] for row_offset in offsets],
            axis=1,
        )
        window_slice = stacked[
            ...,
            2 + column_offset * dilation_rate : 2 + column_offset * dilation_rate + column_count,
        ]
        term = jnp.einsum(
            "oi,bsirw->bsorw", weight, window_slice, preferred_element_type=jnp.float32
        )
        total = term if total is None else total + term
    return total


def choose_rows(block, select):
    masked = jnp.where(select[None, :, None, None, None], block, jnp.zeros_like(block))
    return jnp.sum(masked, axis=1)


def logistic(value):
    return 0.5 + 0.5 * jnp.tanh(0.5 * value)


def rep_sum(part):
    reps = lax.axis_size("rep")
    total = part
    for step in range(1, reps):
        total = total + lax.ppermute(part, "rep", [(r, (r + step) % reps) for r in range(reps)])
    return total


def exchange_sum(part, owned):
    bands = lax.axis_size("band")
    band = lax.axis_index("band")
    total = None
    for shift in range(bands):
        target = (band + shift) % bands
        chunk = lax.dynamic_slice_in_dim(part, target * owned, owned, 0)
        if shift:
            perm = [(b, (b + shift) % bands) for b in range(bands)]
            chunk = lax.ppermute(chunk, "band", perm)
        total = chunk if total is None else total + chunk
    return total


def shards(
    features,
    state,
    live,
    neighbours,
    coarse_perm,
    coarse_state,
    w_update,
    b_update,
    w_reset,
    b_reset,
    w_cand,
    b_cand,
    u_pool,
    u_state,
    b_coarse,
):
    reps = lax.axis_size("rep")
    rep = lax.axis_index("rep")
    per_core = features.shape[0] // reps
    features = lax.dynamic_slice_in_dim(features, rep * per_core, per_core, 0)
    state = lax.dynamic_slice_in_dim(state, rep * per_core, per_core, 0)
    slots = state.shape[1]
    chans = state.shape[2]
    row_count = state.shape[3]
    column_count = state.shape[4]
    inputs_count = features.shape[2]
    half = chans // lax.axis_size("rep")
    start = lax.axis_index("rep") * half
    base = lax.axis_index("tiles") * slots
    ups = neighbours[:, 0]
    downs = neighbours[:, 1]
    up_here = (ups >= base) & (ups < base + slots)
    down_here = (downs >= base) & (downs < base + slots)
    up_far = (ups >= 0) & jnp.logical_not(up_here)
    down_far = (downs >= 0) & jnp.logical_not(down_here)
    alive = live > 0
    first_sel = alive & jnp.logical_not(up_here)
    last_sel = alive & jnp.logical_not(down_here)

    def own_out(filter_weight):
        return lax.dynamic_slice_in_dim(filter_weight, start, half, 1)

    def own_bias(bias):
        return lax.dynamic_slice_in_dim(bias, start, half, 0)[:, None, None]

    hb = state.astype(jnp.bfloat16)
    joined = jnp.concatenate([features, hb], axis=2)
    top = choose_rows(joined[:, :, :, :3, :], first_sel)
    bottom = choose_rows(joined[:, :, :, row_count - 3 :, :], last_sel)
    cycle = padded(jnp.concatenate([top, bottom], axis=2), (("tiles", 2),), 3)
    cycle_prev = cycle[:, None, :, :3, :]
    cycle_next = cycle[:, None, :, 3 * 3 : 4 * 3, :]
    top_local = jnp.take(
        joined[:, :, :, row_count - 3 :, :], jnp.clip(ups - base, 0, slots - 1), axis=1
    )
    bottom_local = jnp.take(joined[:, :, :, :3, :], jnp.clip(downs - base, 0, slots - 1), axis=1)
    zeros_rows = jnp.zeros_like(top_local)
    top = jnp.where(
        up_here[None, :, None, None, None],
        top_local,
        jnp.where(up_far[None, :, None, None, None], cycle_prev + zeros_rows, zeros_rows),
    )
    bottom = jnp.where(
        down_here[None, :, None, None, None],
        bottom_local,
        jnp.where(down_far[None, :, None, None, None], cycle_next + zeros_rows, zeros_rows),
    )
    full = jnp.concatenate([top, joined, bottom], axis=3)
    first = jnp.pad(full, ((0, 0), (0, 0), (0, 0), (0, 0), (2, 2)))
    gates = logistic(
        apply_filter(
            first,
            jnp.concatenate([w_update, w_reset], axis=1),
            1,
            1,
            row_count + 4,
            column_count,
        )
        + jnp.concatenate([b_update, b_reset])[:, None, None]
    )
    update = gates[:, :, :chans, 2 : row_count + 2]
    reset = gates[:, :, chans:]
    hidden_wide = first[:, :, inputs_count:, 1 : row_count + 5, 2 : column_count + 2]
    gated = (reset * hidden_wide.astype(jnp.float32)).astype(jnp.bfloat16)
    gated_pad = jnp.pad(gated, ((0, 0), (0, 0), (0, 0), (0, 0), (2, 2)))
    second = jnp.concatenate([first[:, :, :inputs_count, 1 : row_count + 5, :], gated_pad], axis=2)
    candidate = jnp.tanh(
        apply_filter(second, w_cand, 2, 2, row_count, column_count) + b_cand[:, None, None]
    )
    live_scale = alive.astype(jnp.float32)[None, :, None, None, None]
    new_state = ((1.0 - update) * state + update * candidate) * live_scale
    groups = []
    for step in range(reps):
        piece = lax.dynamic_slice_in_dim(new_state, ((rep + step) % reps) * half, half, 2)
        if step:
            piece = lax.ppermute(piece, "rep", [(r, (r + step) % reps) for r in range(reps)])
        groups.append(piece)
    new_half = jnp.concatenate(
        [
            sum(
                jnp.where((rep - step) % reps == owner, piece, jnp.zeros_like(piece))
                for step, piece in enumerate(groups)
            )
            for owner in range(reps)
        ],
        axis=0,
    )
    summed = jnp.sum(new_state, axis=0)
    column_pool = (
        jnp.arange(column_count)[:, None] // 4 == jnp.arange(column_count // 4)[None, :]
    ).astype(jnp.float32)
    cols = jnp.einsum(
        "schw,wj->schj", summed, column_pool, precision=lax.Precision.HIGHEST
    )
    pooled = jnp.sum(
        cols.reshape(slots, chans, row_count // 4, 4, column_count // 4), axis=3
    ) / 16.0
    new_half, chip_pooled = lax.optimization_barrier((new_half, rep_sum(pooled)))
    ordered = jnp.take(chip_pooled, coarse_perm[0], axis=0)
    part = jnp.einsum("oc,kcij->koij", u_pool, ordered, precision=lax.Precision.HIGHEST)
    pre = exchange_sum(part, coarse_state.shape[0])
    pre = pre + jnp.einsum("oc,kcij->koij", u_state, coarse_state, precision=lax.Precision.HIGHEST)
    pre = pre + b_coarse[None, :, None, None]
    coarse_next = coarse_state + jnp.tanh(pre)
    return (new_half, coarse_next)


def solution(mesh):
    return jax.shard_map(
        shards,
        mesh=mesh,
        in_specs=(
            P(("groups", "band"), "tiles", None, None, None),
            P(("groups", "band"), "tiles", None, None, None),
            P("tiles"),
            P("tiles", None),
            P("tiles", None),
            P(("groups", "tiles", "band"), None, None, None),
            P(),
            P(),
            P(),
            P(),
            P(),
            P(),
            P(),
            P(),
            P(),
        ),
        out_specs=(
            P(("groups", "band"), "tiles", "rep", None, None),
            P(("groups", "tiles", "band"), None, None, None),
        ),
        check_vma=False,
    )
```

```python
import jax
import jax.numpy as jnp
from jax import lax
from jax.sharding import PartitionSpec as P


def padded(block, sides, width):
    for axis, dim in sides:
        count = lax.axis_size(axis)
        forward = [(i, i + 1) for i in range(count - 1)]
        backward = [(target, source) for source, target in forward]
        low = lax.ppermute(
            lax.slice_in_dim(block, block.shape[dim] - width, None, axis=dim), axis, forward
        )
        high = lax.ppermute(lax.slice_in_dim(block, 0, width, axis=dim), axis, backward)
        block = jnp.concatenate([low, block, high], axis=dim)
    return block


def apply_filter(
    padded_input, filter_weight, dilation_rate, first_row_index, row_count, column_count
):
    offsets = (-1, 0, 1)
    stacked = jnp.concatenate(
        [
            padded_input[
                :,
                :,
                :,
                first_row_index
                + row_offset * dilation_rate : first_row_index
                + row_offset * dilation_rate
                + row_count,
                :,
            ]
            for row_offset in offsets
        ],
        axis=2,
    )
    total = None
    for column_offset in offsets:
        weight = jnp.concatenate(
            [filter_weight[(row_offset + 1) * 3 + (column_offset + 1)] for row_offset in offsets],
            axis=1,
        )
        window_slice = stacked[
            ...,
            2 + column_offset * dilation_rate : 2 + column_offset * dilation_rate + column_count,
        ]
        term = jnp.einsum(
            "oi,bsirw->bsorw", weight, window_slice, preferred_element_type=jnp.float32
        )
        total = term if total is None else total + term
    return total


def choose_rows(block, select):
    masked = jnp.where(select[None, :, None, None, None], block, jnp.zeros_like(block))
    return jnp.sum(masked, axis=1)


def logistic(value):
    return 0.5 + 0.5 * jnp.tanh(0.5 * value)


def rep_sum(part):
    reps = lax.axis_size("rep")
    total = part
    for step in range(1, reps):
        total = total + lax.ppermute(part, "rep", [(r, (r + step) % reps) for r in range(reps)])
    return total


def exchange_sum(part, owned):
    bands = lax.axis_size("band")
    band = lax.axis_index("band")
    total = None
    for shift in range(bands):
        target = (band + shift) % bands
        chunk = lax.dynamic_slice_in_dim(part, target * owned, owned, 0)
        if shift:
            perm = [(b, (b + shift) % bands) for b in range(bands)]
            chunk = lax.ppermute(chunk, "band", perm)
        total = chunk if total is None else total + chunk
    return total


def shards(
    features,
    state,
    live,
    neighbours,
    coarse_perm,
    coarse_state,
    w_update,
    b_update,
    w_reset,
    b_reset,
    w_cand,
    b_cand,
    u_pool,
    u_state,
    b_coarse,
):
    reps = lax.axis_size("rep")
    rep = lax.axis_index("rep")
    per_core = features.shape[0] // reps
    features = lax.dynamic_slice_in_dim(features, rep * per_core, per_core, 0)
    state = lax.dynamic_slice_in_dim(state, rep * per_core, per_core, 0)
    slots = state.shape[1]
    chans = state.shape[2]
    row_count = state.shape[3]
    column_count = state.shape[4]
    inputs_count = features.shape[2]
    half = chans // lax.axis_size("rep")
    start = lax.axis_index("rep") * half
    base = lax.axis_index("tiles") * slots
    ups = neighbours[:, 0]
    downs = neighbours[:, 1]
    up_here = (ups >= base) & (ups < base + slots)
    down_here = (downs >= base) & (downs < base + slots)
    up_far = (ups >= 0) & jnp.logical_not(up_here)
    down_far = (downs >= 0) & jnp.logical_not(down_here)
    alive = live > 0
    first_sel = alive & jnp.logical_not(up_here)
    last_sel = alive & jnp.logical_not(down_here)

    def own_out(filter_weight):
        return lax.dynamic_slice_in_dim(filter_weight, start, half, 1)

    def own_bias(bias):
        return lax.dynamic_slice_in_dim(bias, start, half, 0)[:, None, None]

    hb = state.astype(jnp.bfloat16)
    joined = jnp.concatenate([features, hb], axis=2)
    top = choose_rows(joined[:, :, :, :3, :], first_sel)
    bottom = choose_rows(joined[:, :, :, row_count - 3 :, :], last_sel)
    cycle = padded(jnp.concatenate([top, bottom], axis=2), (("tiles", 2),), 3)
    cycle_prev = cycle[:, None, :, :3, :]
    cycle_next = cycle[:, None, :, 3 * 3 : 4 * 3, :]
    top_local = jnp.take(
        joined[:, :, :, row_count - 3 :, :], jnp.clip(ups - base, 0, slots - 1), axis=1
    )
    bottom_local = jnp.take(joined[:, :, :, :3, :], jnp.clip(downs - base, 0, slots - 1), axis=1)
    zeros_rows = jnp.zeros_like(top_local)
    top = jnp.where(
        up_here[None, :, None, None, None],
        top_local,
        jnp.where(up_far[None, :, None, None, None], cycle_prev + zeros_rows, zeros_rows),
    )
    bottom = jnp.where(
        down_here[None, :, None, None, None],
        bottom_local,
        jnp.where(down_far[None, :, None, None, None], cycle_next + zeros_rows, zeros_rows),
    )
    full = jnp.concatenate([top, joined, bottom], axis=3)
    first = jnp.pad(full, ((0, 0), (0, 0), (0, 0), (0, 0), (2, 2)))
    gates = logistic(
        apply_filter(
            first,
            jnp.concatenate([w_update, w_reset], axis=1),
            1,
            1,
            row_count + 4,
            column_count,
        )
        + jnp.concatenate([b_update, b_reset])[:, None, None]
    )
    update = gates[:, :, :chans, 2 : row_count + 2]
    reset = gates[:, :, chans:]
    hidden_wide = first[:, :, inputs_count:, 1 : row_count + 5, 2 : column_count + 2]
    gated = (reset * hidden_wide.astype(jnp.float32)).astype(jnp.bfloat16)
    gated_pad = jnp.pad(gated, ((0, 0), (0, 0), (0, 0), (0, 0), (2, 2)))
    second = jnp.concatenate([first[:, :, :inputs_count, 1 : row_count + 5, :], gated_pad], axis=2)
    candidate = jnp.tanh(
        apply_filter(second, w_cand, 2, 2, row_count, column_count) + b_cand[:, None, None]
    )
    live_scale = alive.astype(jnp.float32)[None, :, None, None, None]
    new_state = ((1.0 - update) * state + update * candidate) * live_scale
    groups = []
    for step in range(reps):
        piece = lax.dynamic_slice_in_dim(new_state, ((rep + step) % reps) * half, half, 2)
        if step:
            piece = lax.ppermute(piece, "rep", [(r, (r + step) % reps) for r in range(reps)])
        groups.append(piece)
    new_half = jnp.concatenate(
        [
            sum(
                jnp.where((rep - step) % reps == owner, piece, jnp.zeros_like(piece))
                for step, piece in enumerate(groups)
            )
            for owner in range(reps)
        ],
        axis=0,
    )
    summed = jnp.sum(new_state, axis=0)
    column_pool = (
        jnp.arange(column_count)[:, None] // 4 == jnp.arange(column_count // 4)[None, :]
    ).astype(jnp.float32)
    cols = jnp.einsum(
        "schw,wj->schj", summed, column_pool, precision=lax.Precision.HIGHEST
    )
    pooled = jnp.sum(
        cols.reshape(slots, chans, row_count // 4, 4, column_count // 4), axis=3
    ) / 16.0
    ordered = jnp.take(pooled, coarse_perm[0], axis=0)
    part = jnp.einsum("oc,kcij->koij", u_pool, ordered, precision=lax.Precision.HIGHEST)
    new_half, band_part = lax.optimization_barrier(
        (new_half, exchange_sum(part, coarse_state.shape[0]))
    )
    pre = rep_sum(band_part)
    pre = pre + jnp.einsum("oc,kcij->koij", u_state, coarse_state, precision=lax.Precision.HIGHEST)
    pre = pre + b_coarse[None, :, None, None]
    coarse_next = coarse_state + jnp.tanh(pre)
    return (new_half, coarse_next)


def solution(mesh):
    return jax.shard_map(
        shards,
        mesh=mesh,
        in_specs=(
            P(("groups", "band"), "tiles", None, None, None),
            P(("groups", "band"), "tiles", None, None, None),
            P("tiles"),
            P("tiles", None),
            P("tiles", None),
            P(("groups", "tiles", "band"), None, None, None),
            P(),
            P(),
            P(),
            P(),
            P(),
            P(),
            P(),
            P(),
            P(),
        ),
        out_specs=(
            P(("groups", "band"), "tiles", "rep", None, None),
            P(("groups", "tiles", "band"), None, None, None),
        ),
        check_vma=False,
    )
```

```python
import jax
import jax.numpy as jnp
from jax import lax
from jax.sharding import PartitionSpec as P


def padded(block, sides, width):
    for axis, dim in sides:
        count = lax.axis_size(axis)
        forward = [(i, i + 1) for i in range(count - 1)]
        backward = [(target, source) for source, target in forward]
        low = lax.ppermute(
            lax.slice_in_dim(block, block.shape[dim] - width, None, axis=dim), axis, forward
        )
        high = lax.ppermute(lax.slice_in_dim(block, 0, width, axis=dim), axis, backward)
        block = jnp.concatenate([low, block, high], axis=dim)
    return block


def apply_filter(
    padded_input, filter_weight, dilation_rate, first_row_index, row_count, column_count
):
    offsets = (-1, 0, 1)
    stacked = jnp.concatenate(
        [
            padded_input[
                :,
                :,
                :,
                first_row_index
                + row_offset * dilation_rate : first_row_index
                + row_offset * dilation_rate
                + row_count,
                :,
            ]
            for row_offset in offsets
        ],
        axis=2,
    )
    total = None
    for column_offset in offsets:
        weight = jnp.concatenate(
            [filter_weight[(row_offset + 1) * 3 + (column_offset + 1)] for row_offset in offsets],
            axis=1,
        )
        window_slice = stacked[
            ...,
            2 + column_offset * dilation_rate : 2 + column_offset * dilation_rate + column_count,
        ]
        term = jnp.einsum(
            "oi,bsirw->bsorw", weight, window_slice, preferred_element_type=jnp.float32
        )
        total = term if total is None else total + term
    return total


def choose_rows(block, select):
    masked = jnp.where(select[None, :, None, None, None], block, jnp.zeros_like(block))
    return jnp.sum(masked, axis=1)


def logistic(value):
    return 0.5 + 0.5 * jnp.tanh(0.5 * value)


def rep_sum(part):
    reps = lax.axis_size("rep")
    total = part
    for step in range(1, reps):
        total = total + lax.ppermute(part, "rep", [(r, (r + step) % reps) for r in range(reps)])
    return total


def exchange_sum(part, owned):
    bands = lax.axis_size("band")
    band = lax.axis_index("band")
    total = None
    for shift in range(bands):
        target = (band + shift) % bands
        chunk = lax.dynamic_slice_in_dim(part, target * owned, owned, 0)
        if shift:
            perm = [(b, (b + shift) % bands) for b in range(bands)]
            chunk = lax.ppermute(chunk, "band", perm)
        total = chunk if total is None else total + chunk
    return total


def shards(
    features,
    state,
    live,
    neighbours,
    coarse_perm,
    coarse_state,
    w_update,
    b_update,
    w_reset,
    b_reset,
    w_cand,
    b_cand,
    u_pool,
    u_state,
    b_coarse,
):
    reps = lax.axis_size("rep")
    rep = lax.axis_index("rep")
    per_core = features.shape[0] // reps
    features = lax.dynamic_slice_in_dim(features, rep * per_core, per_core, 0)
    state = lax.dynamic_slice_in_dim(state, rep * per_core, per_core, 0)
    slots = state.shape[1]
    chans = state.shape[2]
    row_count = state.shape[3]
    column_count = state.shape[4]
    inputs_count = features.shape[2]
    half = chans // lax.axis_size("rep")
    start = lax.axis_index("rep") * half
    base = lax.axis_index("tiles") * slots
    ups = neighbours[:, 0]
    downs = neighbours[:, 1]
    up_here = (ups >= base) & (ups < base + slots)
    down_here = (downs >= base) & (downs < base + slots)
    up_far = (ups >= 0) & jnp.logical_not(up_here)
    down_far = (downs >= 0) & jnp.logical_not(down_here)
    alive = live > 0
    first_sel = alive & jnp.logical_not(up_here)
    last_sel = alive & jnp.logical_not(down_here)

    def own_out(filter_weight):
        return lax.dynamic_slice_in_dim(filter_weight, start, half, 1)

    def own_bias(bias):
        return lax.dynamic_slice_in_dim(bias, start, half, 0)[:, None, None]

    hb = state.astype(jnp.bfloat16)
    joined = jnp.concatenate([features, hb], axis=2)
    top = choose_rows(joined[:, :, :, :3, :], first_sel)
    bottom = choose_rows(joined[:, :, :, row_count - 3 :, :], last_sel)
    cycle = padded(jnp.concatenate([top, bottom], axis=2), (("tiles", 2),), 3)
    cycle_prev = cycle[:, None, :, :3, :]
    cycle_next = cycle[:, None, :, 3 * 3 : 4 * 3, :]
    top_local = jnp.take(
        joined[:, :, :, row_count - 3 :, :], jnp.clip(ups - base, 0, slots - 1), axis=1
    )
    bottom_local = jnp.take(joined[:, :, :, :3, :], jnp.clip(downs - base, 0, slots - 1), axis=1)
    zeros_rows = jnp.zeros_like(top_local)
    top = jnp.where(
        up_here[None, :, None, None, None],
        top_local,
        jnp.where(up_far[None, :, None, None, None], cycle_prev + zeros_rows, zeros_rows),
    )
    bottom = jnp.where(
        down_here[None, :, None, None, None],
        bottom_local,
        jnp.where(down_far[None, :, None, None, None], cycle_next + zeros_rows, zeros_rows),
    )
    full = jnp.concatenate([top, joined, bottom], axis=3)
    first = jnp.pad(full, ((0, 0), (0, 0), (0, 0), (0, 0), (2, 2)))
    gates = logistic(
        apply_filter(
            first,
            jnp.concatenate([w_update, w_reset], axis=1),
            1,
            1,
            row_count + 4,
            column_count,
        )
        + jnp.concatenate([b_update, b_reset])[:, None, None]
    )
    update = gates[:, :, :chans, 2 : row_count + 2]
    reset = gates[:, :, chans:]
    hidden_wide = first[:, :, inputs_count:, 1 : row_count + 5, 2 : column_count + 2]
    gated = (reset * hidden_wide.astype(jnp.float32)).astype(jnp.bfloat16)
    gated_pad = jnp.pad(gated, ((0, 0), (0, 0), (0, 0), (0, 0), (2, 2)))
    second = jnp.concatenate([first[:, :, :inputs_count, 1 : row_count + 5, :], gated_pad], axis=2)
    candidate = jnp.tanh(
        apply_filter(second, w_cand, 2, 2, row_count, column_count) + b_cand[:, None, None]
    )
    live_scale = alive.astype(jnp.float32)[None, :, None, None, None]
    new_state = ((1.0 - update) * state + update * candidate) * live_scale
    groups = []
    for step in range(reps):
        piece = lax.dynamic_slice_in_dim(new_state, ((rep + step) % reps) * half, half, 2)
        if step:
            piece = lax.ppermute(piece, "rep", [(r, (r + step) % reps) for r in range(reps)])
        groups.append(piece)
    new_half = jnp.concatenate(
        [
            sum(
                jnp.where((rep - step) % reps == owner, piece, jnp.zeros_like(piece))
                for step, piece in enumerate(groups)
            )
            for owner in range(reps)
        ],
        axis=0,
    )
    summed = jnp.sum(new_state, axis=0)
    column_pool = (
        jnp.arange(column_count)[:, None] // 4 == jnp.arange(column_count // 4)[None, :]
    ).astype(jnp.float32)
    cols = jnp.einsum(
        "schw,wj->schj", summed, column_pool, precision=lax.Precision.HIGHEST
    )
    pooled = jnp.sum(
        cols.reshape(slots, chans, row_count // 4, 4, column_count // 4), axis=3
    ) / 16.0
    bands = lax.axis_size("band")
    band_pooled = pooled
    for shift in range(1, bands):
        band_pooled = band_pooled + lax.ppermute(
            pooled, "band", [(b, (b + shift) % bands) for b in range(bands)]
        )
    owned = coarse_state.shape[0]
    mine = lax.dynamic_slice_in_dim(coarse_perm[0], lax.axis_index("band") * owned, owned, 0)
    ordered = jnp.take(band_pooled, mine, axis=0)
    part = jnp.einsum("oc,kcij->koij", u_pool, ordered, precision=lax.Precision.HIGHEST)
    new_half, part = lax.optimization_barrier((new_half, part))
    pre = rep_sum(part)
    pre = pre + jnp.einsum("oc,kcij->koij", u_state, coarse_state, precision=lax.Precision.HIGHEST)
    pre = pre + b_coarse[None, :, None, None]
    coarse_next = coarse_state + jnp.tanh(pre)
    return (new_half, coarse_next)


def solution(mesh):
    return jax.shard_map(
        shards,
        mesh=mesh,
        in_specs=(
            P(("groups", "band"), "tiles", None, None, None),
            P(("groups", "band"), "tiles", None, None, None),
            P("tiles"),
            P("tiles", None),
            P("tiles", None),
            P(("groups", "tiles", "band"), None, None, None),
            P(),
            P(),
            P(),
            P(),
            P(),
            P(),
            P(),
            P(),
            P(),
        ),
        out_specs=(
            P(("groups", "band"), "tiles", "rep", None, None),
            P(("groups", "tiles", "band"), None, None, None),
        ),
        check_vma=False,
    )
```

```python
import jax
import jax.numpy as jnp
from jax import lax
from jax.sharding import PartitionSpec as P


def padded(block, sides, width):
    for axis, dim in sides:
        count = lax.axis_size(axis)
        forward = [(i, i + 1) for i in range(count - 1)]
        backward = [(target, source) for source, target in forward]
        low = lax.ppermute(
            lax.slice_in_dim(block, block.shape[dim] - width, None, axis=dim), axis, forward
        )
        high = lax.ppermute(lax.slice_in_dim(block, 0, width, axis=dim), axis, backward)
        block = jnp.concatenate([low, block, high], axis=dim)
    return block


def apply_filter(
    padded_input, filter_weight, dilation_rate, first_row_index, row_count, column_count
):
    offsets = (-1, 0, 1)
    stacked = jnp.concatenate(
        [
            padded_input[
                :,
                :,
                :,
                first_row_index
                + row_offset * dilation_rate : first_row_index
                + row_offset * dilation_rate
                + row_count,
                :,
            ]
            for row_offset in offsets
        ],
        axis=2,
    )
    total = None
    for column_offset in offsets:
        weight = jnp.concatenate(
            [filter_weight[(row_offset + 1) * 3 + (column_offset + 1)] for row_offset in offsets],
            axis=1,
        )
        window_slice = stacked[
            ...,
            2 + column_offset * dilation_rate : 2 + column_offset * dilation_rate + column_count,
        ]
        term = jnp.einsum(
            "oi,bsirw->bsorw", weight, window_slice, preferred_element_type=jnp.float32
        )
        total = term if total is None else total + term
    return total


def choose_rows(block, select):
    masked = jnp.where(select[None, :, None, None, None], block, jnp.zeros_like(block))
    return jnp.sum(masked, axis=1)


def logistic(value):
    return 0.5 + 0.5 * jnp.tanh(0.5 * value)


def rep_sum(part):
    reps = lax.axis_size("rep")
    total = part
    for step in range(1, reps):
        total = total + lax.ppermute(part, "rep", [(r, (r + step) % reps) for r in range(reps)])
    return total


def exchange_sum(make_chunk):
    bands = lax.axis_size("band")
    band = lax.axis_index("band")
    total = None
    for shift in list(range(1, bands)) + [0]:
        chunk = make_chunk((band + shift) % bands)
        if shift:
            perm = [(b, (b + shift) % bands) for b in range(bands)]
            chunk = lax.ppermute(chunk, "band", perm)
        total = chunk if total is None else total + chunk
    return total


def shards(
    features,
    state,
    live,
    neighbours,
    coarse_perm,
    coarse_state,
    w_update,
    b_update,
    w_reset,
    b_reset,
    w_cand,
    b_cand,
    u_pool,
    u_state,
    b_coarse,
):
    reps = lax.axis_size("rep")
    rep = lax.axis_index("rep")
    per_core = features.shape[0] // reps
    features = lax.dynamic_slice_in_dim(features, rep * per_core, per_core, 0)
    state = lax.dynamic_slice_in_dim(state, rep * per_core, per_core, 0)
    slots = state.shape[1]
    chans = state.shape[2]
    row_count = state.shape[3]
    column_count = state.shape[4]
    inputs_count = features.shape[2]
    half = chans // lax.axis_size("rep")
    start = lax.axis_index("rep") * half
    base = lax.axis_index("tiles") * slots
    ups = neighbours[:, 0]
    downs = neighbours[:, 1]
    up_here = (ups >= base) & (ups < base + slots)
    down_here = (downs >= base) & (downs < base + slots)
    up_far = (ups >= 0) & jnp.logical_not(up_here)
    down_far = (downs >= 0) & jnp.logical_not(down_here)
    alive = live > 0
    first_sel = alive & jnp.logical_not(up_here)
    last_sel = alive & jnp.logical_not(down_here)

    def own_out(filter_weight):
        return lax.dynamic_slice_in_dim(filter_weight, start, half, 1)

    def own_bias(bias):
        return lax.dynamic_slice_in_dim(bias, start, half, 0)[:, None, None]

    hb = state.astype(jnp.bfloat16)
    joined = jnp.concatenate([features, hb], axis=2)
    top = choose_rows(joined[:, :, :, :3, :], first_sel)
    bottom = choose_rows(joined[:, :, :, row_count - 3 :, :], last_sel)
    cycle = padded(jnp.concatenate([top, bottom], axis=2), (("tiles", 2),), 3)
    cycle_prev = cycle[:, None, :, :3, :]
    cycle_next = cycle[:, None, :, 3 * 3 : 4 * 3, :]
    top_local = jnp.take(
        joined[:, :, :, row_count - 3 :, :], jnp.clip(ups - base, 0, slots - 1), axis=1
    )
    bottom_local = jnp.take(joined[:, :, :, :3, :], jnp.clip(downs - base, 0, slots - 1), axis=1)
    zeros_rows = jnp.zeros_like(top_local)
    top = jnp.where(
        up_here[None, :, None, None, None],
        top_local,
        jnp.where(up_far[None, :, None, None, None], cycle_prev + zeros_rows, zeros_rows),
    )
    bottom = jnp.where(
        down_here[None, :, None, None, None],
        bottom_local,
        jnp.where(down_far[None, :, None, None, None], cycle_next + zeros_rows, zeros_rows),
    )
    full = jnp.concatenate([top, joined, bottom], axis=3)
    first = jnp.pad(full, ((0, 0), (0, 0), (0, 0), (0, 0), (2, 2)))
    gates = logistic(
        apply_filter(
            first,
            jnp.concatenate([w_update, w_reset], axis=1),
            1,
            1,
            row_count + 4,
            column_count,
        )
        + jnp.concatenate([b_update, b_reset])[:, None, None]
    )
    update = gates[:, :, :chans, 2 : row_count + 2]
    reset = gates[:, :, chans:]
    hidden_wide = first[:, :, inputs_count:, 1 : row_count + 5, 2 : column_count + 2]
    gated = (reset * hidden_wide.astype(jnp.float32)).astype(jnp.bfloat16)
    gated_pad = jnp.pad(gated, ((0, 0), (0, 0), (0, 0), (0, 0), (2, 2)))
    second = jnp.concatenate([first[:, :, :inputs_count, 1 : row_count + 5, :], gated_pad], axis=2)
    candidate = jnp.tanh(
        apply_filter(second, w_cand, 2, 2, row_count, column_count) + b_cand[:, None, None]
    )
    live_scale = alive.astype(jnp.float32)[None, :, None, None, None]
    new_state = ((1.0 - update) * state + update * candidate) * live_scale
    groups = []
    for step in range(reps):
        piece = lax.dynamic_slice_in_dim(new_state, ((rep + step) % reps) * half, half, 2)
        if step:
            piece = lax.ppermute(piece, "rep", [(r, (r + step) % reps) for r in range(reps)])
        groups.append(piece)
    new_half = jnp.concatenate(
        [
            sum(
                jnp.where((rep - step) % reps == owner, piece, jnp.zeros_like(piece))
                for step, piece in enumerate(groups)
            )
            for owner in range(reps)
        ],
        axis=0,
    )
    summed = jnp.sum(new_state, axis=0)
    column_pool = (
        jnp.arange(column_count)[:, None] // 4 == jnp.arange(column_count // 4)[None, :]
    ).astype(jnp.float32)
    cols = jnp.einsum(
        "schw,wj->schj", summed, column_pool, precision=lax.Precision.HIGHEST
    )
    pooled = jnp.sum(
        cols.reshape(slots, chans, row_count // 4, 4, column_count // 4), axis=3
    ) / 16.0
    owned = coarse_state.shape[0]

    def make_chunk(target):
        picked = lax.dynamic_slice_in_dim(coarse_perm[0], target * owned, owned, 0)
        ordered = jnp.take(pooled, picked, axis=0)
        return jnp.einsum("oc,kcij->koij", u_pool, ordered, precision=lax.Precision.HIGHEST)

    new_half, band_part = lax.optimization_barrier((new_half, exchange_sum(make_chunk)))
    pre = rep_sum(band_part)
    pre = pre + jnp.einsum("oc,kcij->koij", u_state, coarse_state, precision=lax.Precision.HIGHEST)
    pre = pre + b_coarse[None, :, None, None]
    coarse_next = coarse_state + jnp.tanh(pre)
    return (new_half, coarse_next)


def solution(mesh):
    return jax.shard_map(
        shards,
        mesh=mesh,
        in_specs=(
            P(("groups", "band"), "tiles", None, None, None),
            P(("groups", "band"), "tiles", None, None, None),
            P("tiles"),
            P("tiles", None),
            P("tiles", None),
            P(("groups", "tiles", "band"), None, None, None),
            P(),
            P(),
            P(),
            P(),
            P(),
            P(),
            P(),
            P(),
            P(),
        ),
        out_specs=(
            P(("groups", "band"), "tiles", "rep", None, None),
            P(("groups", "tiles", "band"), None, None, None),
        ),
        check_vma=False,
    )
```
